32 devices in a mesh: cell: 4 (over y, x), blk: 8 (over z, core).
Axes of the slice: x: 2, y: 2, z: 4, core: 2. Of those that a mesh axis runs over, the one named last changes fastest.
Arguments:
- codes: bfloat16 [16384, 128], P(('cell', 'blk')), may hold values from -60 to 60
- scales: float32 [16384], P(('cell', 'blk')), may hold values from 0.5 to 2
- coarse_ids: int32 [16384], P(('cell', 'blk')), may hold values from 0 to 3, as said below
- centroids: bfloat16 [32768, 128], P(('cell', 'blk')), may hold values from -6 to 6
Outputs:
- reconstruction: bfloat16 [16384, 128], P(('cell', 'blk'))
- residual: bfloat16 [16384, 128], P(('cell', 'blk'))
The draws below stay inside these ranges and needn't reach their ends.
Inputs may be any that keep to these rules, and one draw needn't show every extreme that they name: `coarse_ids`: on every device, the number of its 512 rows that name partition g is the same for all devices; at most 256 rows of one device name one partition, and one partition is named by exactly 256 rows of every device.
All inputs are finite; a program needn't handle non-finite values.
Results may differ from the reference program's by a relative error of at most 0.006.
Values may be sent and summed in bfloat16 or wider, within the bound.
No kernel may reach another device: no remote copies, remote signals or barrier semaphores. Data moves between devices by JAX's collectives and lax.ppermute only.
A program may use at most 256 MiB of HBM per device.

```python
import math
import jax
import jax.numpy as jnp
from jax import lax

D = 128
CENT_DEV = 1024
ROWS_DEV = 512
CENTROIDS = 32768
TOKENS = 16384
N_CELL = 4
N_BLK = 8


def loop_counts(key):
    loops = N_CELL
    cap = 2 * ROWS_DEV // loops
    rest = ROWS_DEV - cap
    base = rest // (loops - 1)
    extra = rest - base * (loops - 1)
    first, second = jax.random.split(jax.random.fold_in(key, 101))
    hot = jax.random.randint(first, (), 0, loops)
    shifts = jax.random.randint(second, (loops - 1,), 0, base // 2 + 1)
    others = base + shifts - jnp.roll(shifts, 1) + (jnp.arange(loops - 1) < extra).astype(jnp.int32)
    index = jnp.arange(loops, dtype=jnp.int32)
    picked = jnp.take(others, jnp.clip(index - (index > hot).astype(jnp.int32), 0, loops - 2))
    return jnp.where(index == hot, cap, picked).astype(jnp.int32)


def coarse_draw(key):
    bounds = jnp.cumsum(loop_counts(key))
    place = jnp.arange(ROWS_DEV, dtype=jnp.int32)
    sequence = jnp.sum((place[:, None] >= bounds[None, :]).astype(jnp.int32), axis=1)
    keys = jax.random.split(jax.random.fold_in(key, 102), N_CELL * N_BLK)

    def shuffle(one_key):
        return jax.random.permutation(one_key, ROWS_DEV)
    perms = jax.vmap(shuffle)(keys)
    return sequence[perms].reshape(TOKENS).astype(jnp.int32)


def centroid_draw(key):
    first = jax.random.fold_in(jax.random.fold_in(key, 202), 0)
    return jnp.clip(jax.random.normal(first, (CENTROIDS, D), jnp.float32), -6.0, 6.0)


def draw_coarse_ids(key, part):
    return coarse_draw(key)


def draw_centroids(key, part):
    return centroid_draw(key).astype(jnp.bfloat16)


def draw_codes(key, part):
    first = jax.random.fold_in(key, 303)
    codes = jnp.clip(jax.random.normal(first, (TOKENS, D), jnp.float32), -6.0, 6.0)
    return codes.astype(jnp.bfloat16)


def level_of(own_key, dims, cuts, least, top_value):
    gain, own = 1.0, jax.random.fold_in(own_key, 6)
    for axis_at, parts in cuts:
        heights = jnp.exp(jax.random.uniform(jax.random.fold_in(own, axis_at), (parts,), jnp.float32, least / len(cuts), top_value / len(cuts)))
        gain = gain * jnp.repeat(heights, dims[axis_at] // parts).reshape([-1 if axis == axis_at else 1 for axis in range(len(dims))])
    return gain


def setup_inputs(seed: int = 0) -> dict:
    key_of = jax.random.split(jax.random.key(seed), 5)
    codes = draw_codes(jax.random.fold_in(key_of[4], 71), 0)
    scales = jnp.clip(jnp.exp(math.log(2.0) - 1.3862944 * jax.random.uniform(key_of[1], (TOKENS,), jnp.float32) ** level_of(key_of[1], (TOKENS,), ((0, 32),), -0.2, 0.2)), 0.5, 2.0)
    coarse_ids = draw_coarse_ids(jax.random.fold_in(key_of[4], 71), 0)
    centroids = draw_centroids(jax.random.fold_in(key_of[4], 71), 0)
    return {"codes": codes, "scales": scales, "coarse_ids": coarse_ids, "centroids": centroids}


def reference(codes, scales, coarse_ids, centroids):
    width = codes.shape[1]
    beta = 1.0 / math.sqrt(width)
    loop_size = CENT_DEV * N_BLK
    dequant = (codes.astype(jnp.float32) * scales[:, None]).astype(jnp.bfloat16)
    order = jnp.argsort(coarse_ids, stable=True).astype(jnp.int32)
    sorted_rows = dequant[order]
    sorted_ids = coarse_ids[order]
    block = min(512, TOKENS)
    count_blocks = TOKENS // block
    rows_blocks = sorted_rows.reshape(count_blocks, block, width)
    ids_blocks = sorted_ids.reshape(count_blocks, block)

    def one_block(pair):
        rows, ids = pair

        def per_loop(group, carry):
            slab = lax.dynamic_slice_in_dim(centroids, (group * loop_size).astype(jnp.int32), loop_size, 0)
            scores = jnp.dot(rows, slab.T, preferred_element_type=jnp.float32) * beta
            top = lax.optimization_barrier(jnp.max(scores, axis=1))
            weights = jnp.exp(scores - top[:, None]).astype(jnp.bfloat16)
            total = lax.optimization_barrier(jnp.sum(weights.astype(jnp.float32), axis=1))
            numer = jnp.dot(weights, slab, preferred_element_type=jnp.float32)
            recon = (numer / total[:, None]).astype(jnp.bfloat16)
            return jnp.where((ids == group)[:, None], recon, carry)
        return lax.fori_loop(ids[0], ids[block - 1] + 1, per_loop, jnp.zeros((block, width), jnp.bfloat16))
    recon_sorted = lax.map(one_block, (rows_blocks, ids_blocks)).reshape(TOKENS, width)
    recon = jnp.zeros_like(recon_sorted).at[order].set(recon_sorted)
    residual = (dequant.astype(jnp.float32) - recon.astype(jnp.float32)).astype(jnp.bfloat16)
    return (recon, residual)
```

```python
import functools
import math

import jax
import jax.numpy as jnp
from jax import lax
from jax.experimental import pallas as pl
from jax.experimental.pallas import tpu as pltpu
from jax.sharding import Mesh
from jax.sharding import PartitionSpec as P

ROWS = ("cell", "chip", "core")


def _soft_kernel(q_ref, c_ref, o_ref, m_sc, l_sc, acc_sc, *, chunk, beta):
    n_chunks = c_ref.shape[0] // chunk
    q = q_ref[...]

    def scores(i):
        c = c_ref[pl.ds(pl.multiple_of(i * chunk, chunk), chunk), :]
        s = lax.dot_general(q, c, (((1,), (1,)), ((), ())), preferred_element_type=jnp.float32)
        return s * beta, c

    m_sc[...] = jnp.full(m_sc.shape, -jnp.inf, jnp.float32)

    @pl.loop(0, n_chunks)
    def _(i):
        s, _ = scores(i)
        m_sc[...] = jnp.maximum(m_sc[...], jnp.max(s, axis=1, keepdims=True))

    l_sc[...] = jnp.zeros(l_sc.shape, jnp.float32)
    acc_sc[...] = jnp.zeros(acc_sc.shape, jnp.float32)
    top = m_sc[...]

    @pl.loop(0, n_chunks)
    def _(i):
        s, c = scores(i)
        w = jnp.exp(s - top).astype(jnp.bfloat16)
        l_sc[...] += jnp.sum(w.astype(jnp.float32), axis=1, keepdims=True)
        acc_sc[...] += jnp.dot(w, c, preferred_element_type=jnp.float32)

    o_ref[...] = (acc_sc[...] / l_sc[...]).astype(o_ref.dtype)


def soft_reconstruct(queries, cents, *, tq=256, chunk=512):
    slots, width = queries.shape
    n_cent = cents.shape[0]
    beta = 1.0 / math.sqrt(width)
    flops = 3 * 2 * slots * n_cent * width
    return pl.pallas_call(
        functools.partial(_soft_kernel, chunk=chunk, beta=beta),
        out_shape=jax.ShapeDtypeStruct((slots, width), jnp.bfloat16),
        grid=(slots // tq,),
        in_specs=[
            pl.BlockSpec((tq, width), lambda i: (i, 0)),
            pl.BlockSpec((n_cent, width), lambda i: (0, 0)),
        ],
        out_specs=pl.BlockSpec((tq, width), lambda i: (i, 0)),
        scratch_shapes=[
            pltpu.VMEM((tq, 1), jnp.float32),
            pltpu.VMEM((tq, 1), jnp.float32),
            pltpu.VMEM((tq, width), jnp.float32),
        ],
        compiler_params=pltpu.CompilerParams(vmem_limit_bytes=48 * 1024 * 1024),
        cost_estimate=pl.CostEstimate(
            flops=flops,
            transcendentals=slots * n_cent,
            bytes_accessed=2 * (2 * slots * width + n_cent * width),
        ),
    )(queries, cents)


def local(codes, scales, coarse_ids, centroids):
    rows_dev = codes.shape[0]
    width = codes.shape[1]
    loops = lax.axis_size("cell")
    cap = 2 * rows_dev // loops
    dequant = (codes.astype(jnp.float32) * scales[:, None]).astype(jnp.bfloat16)
    onehot = (coarse_ids[:, None] == jnp.arange(loops, dtype=jnp.int32)[None, :]).astype(jnp.int32)
    ranks = jnp.sum(jnp.cumsum(onehot, axis=0) * onehot, axis=1) - 1
    slots = coarse_ids * cap + ranks
    outgoing = jnp.zeros((loops * cap, width), jnp.bfloat16).at[slots].set(dequant)
    arrived = lax.all_to_all(
        outgoing.reshape(loops, cap, width), "cell", split_axis=0, concat_axis=0, tiled=True
    )
    queries = arrived.reshape(loops * cap, width)
    part = lax.all_gather(centroids, "chip", axis=0, tiled=True)
    part = lax.all_gather(part, "core", axis=0, tiled=True)
    recon = soft_reconstruct(queries, part)
    back = lax.all_to_all(
        recon.reshape(loops, cap, width), "cell", split_axis=0, concat_axis=0, tiled=True
    ).reshape(loops * cap, width)
    mine = back[slots]
    residual = (dequant.astype(jnp.float32) - mine.astype(jnp.float32)).astype(jnp.bfloat16)
    return (mine, residual)


def solution(mesh):
    n_cell = mesh.shape["cell"]
    n_blk = mesh.shape["blk"]
    fine = Mesh(mesh.devices.reshape(n_cell, n_blk // 2, 2), ROWS)
    rows = P(ROWS, None)
    in_specs = (rows, P(ROWS), P(ROWS), rows)
    out_specs = (rows, rows)
    return jax.shard_map(local, mesh=fine, in_specs=in_specs, out_specs=out_specs, check_vma=False)
```

```python
import functools
import math

import jax
import jax.numpy as jnp
from jax import lax
from jax.experimental import pallas as pl
from jax.experimental.pallas import tpu as pltpu
from jax.sharding import PartitionSpec as P


def _soft_kernel(q_ref, c_ref, o_ref, m_sc, l_sc, acc_sc, s_sc, *, chunk, beta):
    n_chunks = c_ref.shape[0] // chunk
    lanes = m_sc.shape[1]
    q = q_ref[...]
    m_sc[...] = jnp.full(m_sc.shape, -jnp.inf, jnp.float32)

    @pl.loop(0, n_chunks)
    def _(i):
        cols = pl.ds(pl.multiple_of(i * chunk, chunk), chunk)
        s = lax.dot_general(
            q, c_ref[cols, :], (((1,), (1,)), ((), ())), preferred_element_type=jnp.float32
        ) * beta
        s_sc[:, cols] = s
        m = m_sc[...]
        for j in range(chunk // lanes):
            m = jnp.maximum(m, s[:, j * lanes:(j + 1) * lanes])
        m_sc[...] = m

    top = jnp.max(m_sc[...], axis=1, keepdims=True)
    l_sc[...] = jnp.zeros(l_sc.shape, jnp.float32)
    acc_sc[...] = jnp.zeros(acc_sc.shape, jnp.float32)

    @pl.loop(0, n_chunks)
    def _(i):
        cols = pl.ds(pl.multiple_of(i * chunk, chunk), chunk)
        w = jnp.exp(s_sc[:, cols] - top).astype(jnp.bfloat16)
        wf = w.astype(jnp.float32)
        l = l_sc[...]
        for j in range(chunk // lanes):
            l = l + wf[:, j * lanes:(j + 1) * lanes]
        l_sc[...] = l
        acc_sc[...] += jnp.dot(w, c_ref[cols, :], preferred_element_type=jnp.float32)

    total = jnp.sum(l_sc[...], axis=1, keepdims=True)
    o_ref[...] = (acc_sc[...] / total).astype(o_ref.dtype)


def soft_reconstruct(queries, cents):
    slots, width = queries.shape
    n_cent = cents.shape[0]
    chunk = min(2048, n_cent)
    tq = min(512, slots, (16 << 20) // (4 * n_cent))
    vmem = 4 * tq * n_cent + 2 * 2 * n_cent * width + 8 * tq * width * 4 + (8 << 20)
    return pl.pallas_call(
        functools.partial(_soft_kernel, chunk=chunk, beta=1.0 / math.sqrt(width)),
        out_shape=jax.ShapeDtypeStruct((slots, width), jnp.bfloat16),
        grid=(slots // tq,),
        in_specs=[
            pl.BlockSpec((tq, width), lambda i: (i, 0)),
            pl.BlockSpec((n_cent, width), lambda i: (0, 0)),
        ],
        out_specs=pl.BlockSpec((tq, width), lambda i: (i, 0)),
        scratch_shapes=[
            pltpu.VMEM((tq, 128), jnp.float32),
            pltpu.VMEM((tq, 128), jnp.float32),
            pltpu.VMEM((tq, width), jnp.float32),
            pltpu.VMEM((tq, n_cent), jnp.float32),
        ],
        compiler_params=pltpu.CompilerParams(vmem_limit_bytes=min(vmem, 60 << 20)),
        cost_estimate=pl.CostEstimate(
            flops=2 * 2 * slots * n_cent * width,
            transcendentals=slots * n_cent,
            bytes_accessed=2 * (2 * slots * width + n_cent * width),
        ),
    )(queries, cents)


def local(codes, scales, coarse_ids, centroids):
    rows_dev = codes.shape[0]
    width = codes.shape[1]
    loops = lax.axis_size("cell")
    cap = 2 * rows_dev // loops
    dequant = (codes.astype(jnp.float32) * scales[:, None]).astype(jnp.bfloat16)
    onehot = (coarse_ids[:, None] == jnp.arange(loops, dtype=jnp.int32)[None, :]).astype(jnp.int32)
    ranks = jnp.sum(jnp.cumsum(onehot, axis=0) * onehot, axis=1) - 1
    slots = coarse_ids * cap + ranks
    outgoing = jnp.zeros((loops * cap, width), jnp.bfloat16).at[slots].set(dequant)
    arrived = lax.all_to_all(
        outgoing.reshape(loops, cap, width), "cell", split_axis=0, concat_axis=0, tiled=True
    )
    queries = arrived.reshape(loops * cap, width)
    part = lax.all_gather(centroids, "blk", axis=0, tiled=True)
    recon = soft_reconstruct(queries, part)
    back = lax.all_to_all(
        recon.reshape(loops, cap, width), "cell", split_axis=0, concat_axis=0, tiled=True
    ).reshape(loops * cap, width)
    mine = back[slots]
    residual = (dequant.astype(jnp.float32) - mine.astype(jnp.float32)).astype(jnp.bfloat16)
    return (mine, residual)


def solution(mesh):
    rows = P(("cell", "blk"), None)
    in_specs = (rows, P(("cell", "blk")), P(("cell", "blk")), rows)
    out_specs = (rows, rows)
    return jax.shard_map(local, mesh=mesh, in_specs=in_specs, out_specs=out_specs, check_vma=False)
```

```python
import functools
import math

import jax
import jax.numpy as jnp
from jax import lax
from jax.experimental import pallas as pl
from jax.experimental.pallas import tpu as pltpu
from jax.sharding import PartitionSpec as P


def _soft_kernel(q_ref, c_ref, o_ref, m_sc, l_sc, acc_sc, s_sc, *, chunk, beta):
    n_chunks = c_ref.shape[0] // chunk
    lanes = m_sc.shape[1]
    q = q_ref[...]
    m_sc[...] = jnp.full(m_sc.shape, -jnp.inf, jnp.float32)

    @pl.loop(0, n_chunks)
    def _(i):
        cols = pl.ds(pl.multiple_of(i * chunk, chunk), chunk)
        s = lax.dot_general(
            q, c_ref[cols, :], (((1,), (1,)), ((), ())), preferred_element_type=jnp.float32
        ) * beta
        s_sc[:, cols] = s
        m = m_sc[...]
        for j in range(chunk // lanes):
            m = jnp.maximum(m, s[:, j * lanes:(j + 1) * lanes])
        m_sc[...] = m

    top = jnp.max(m_sc[...], axis=1, keepdims=True)
    l_sc[...] = jnp.zeros(l_sc.shape, jnp.float32)
    acc_sc[...] = jnp.zeros(acc_sc.shape, jnp.float32)

    @pl.loop(0, n_chunks)
    def _(i):
        cols = pl.ds(pl.multiple_of(i * chunk, chunk), chunk)
        w = jnp.exp(s_sc[:, cols] - top).astype(jnp.bfloat16)
        wf = w.astype(jnp.float32)
        l = l_sc[...]
        for j in range(chunk // lanes):
            l = l + wf[:, j * lanes:(j + 1) * lanes]
        l_sc[...] = l
        acc_sc[...] += jnp.dot(w, c_ref[cols, :], preferred_element_type=jnp.float32)

    total = jnp.sum(l_sc[...], axis=1, keepdims=True)
    o_ref[...] = (acc_sc[...] / total).astype(o_ref.dtype)


def soft_reconstruct(queries, cents):
    slots, width = queries.shape
    n_cent = cents.shape[0]
    chunk = min(2048, n_cent)
    tq = min(512, slots, (16 << 20) // (4 * n_cent))
    vmem = 4 * tq * n_cent + 2 * 2 * n_cent * width + 8 * tq * width * 4 + (8 << 20)
    return pl.pallas_call(
        functools.partial(_soft_kernel, chunk=chunk, beta=1.0 / math.sqrt(width)),
        out_shape=jax.ShapeDtypeStruct((slots, width), jnp.bfloat16),
        grid=(slots // tq,),
        in_specs=[
            pl.BlockSpec((tq, width), lambda i: (i, 0)),
            pl.BlockSpec((n_cent, width), lambda i: (0, 0)),
        ],
        out_specs=pl.BlockSpec((tq, width), lambda i: (i, 0)),
        scratch_shapes=[
            pltpu.VMEM((tq, 128), jnp.float32),
            pltpu.VMEM((tq, 128), jnp.float32),
            pltpu.VMEM((tq, width), jnp.float32),
            pltpu.VMEM((tq, n_cent), jnp.float32),
        ],
        compiler_params=pltpu.CompilerParams(vmem_limit_bytes=min(vmem, 60 << 20)),
        cost_estimate=pl.CostEstimate(
            flops=2 * 2 * slots * n_cent * width,
            transcendentals=slots * n_cent,
            bytes_accessed=2 * (2 * slots * width + n_cent * width),
        ),
    )(queries, cents)


def _shift(x, axis, n, d):
    return lax.ppermute(x, axis, [(i, (i + d) % n) for i in range(n)])


def _gather_partition(centroids):
    n_blk = lax.axis_size("blk")
    n_chip = n_blk // 2
    pieces = [centroids]
    for d in range(1, n_chip):
        pairs = [(k * 2 + c, ((k + d) % n_chip) * 2 + c) for k in range(n_chip) for c in range(2)]
        pieces.append(lax.ppermute(centroids, "blk", pairs))
    half = jnp.concatenate(pieces, axis=0)
    other = lax.ppermute(half, "blk", [(b, b ^ 1) for b in range(n_blk)])
    return jnp.concatenate([half, other], axis=0)


def local(codes, scales, coarse_ids, centroids):
    rows_dev = codes.shape[0]
    width = codes.shape[1]
    loops = lax.axis_size("cell")
    cap = 2 * rows_dev // loops
    me = lax.axis_index("cell")
    dequant = (codes.astype(jnp.float32) * scales[:, None]).astype(jnp.bfloat16)
    onehot = (coarse_ids[:, None] == jnp.arange(loops, dtype=jnp.int32)[None, :]).astype(jnp.int32)
    ranks = jnp.sum(jnp.cumsum(onehot, axis=0) * onehot, axis=1) - 1
    slots = ((coarse_ids - me) % loops) * cap + ranks
    outgoing = jnp.zeros((loops * cap, width), jnp.bfloat16).at[slots].set(dequant)
    outgoing = outgoing.reshape(loops, cap, width)
    part = _gather_partition(centroids)
    arrived = [outgoing[0]] + [_shift(outgoing[d], "cell", loops, d) for d in range(1, loops)]
    queries = jnp.concatenate(arrived, axis=0)
    recon = soft_reconstruct(queries, part).reshape(loops, cap, width)
    back = [recon[0]] + [_shift(recon[d], "cell", loops, -d) for d in range(1, loops)]
    mine = jnp.concatenate(back, axis=0)[slots]
    residual = (dequant.astype(jnp.float32) - mine.astype(jnp.float32)).astype(jnp.bfloat16)
    return (mine, residual)


def solution(mesh):
    rows = P(("cell", "blk"), None)
    in_specs = (rows, P(("cell", "blk")), P(("cell", "blk")), rows)
    out_specs = (rows, rows)
    return jax.shard_map(local, mesh=mesh, in_specs=in_specs, out_specs=out_specs, check_vma=False)
```

```python
import functools
import math

import jax
import jax.numpy as jnp
from jax import lax
from jax.experimental import pallas as pl
from jax.experimental.pallas import tpu as pltpu
from jax.sharding import PartitionSpec as P


def _soft_kernel(q_ref, c_ref, o_ref, m_sc, l_sc, acc_sc, s_sc, *, chunk, beta):
    n_chunks = c_ref.shape[0] // chunk
    lanes = m_sc.shape[1]
    q = q_ref[...]
    m_sc[...] = jnp.full(m_sc.shape, -jnp.inf, jnp.float32)

    @pl.loop(0, n_chunks)
    def _(i):
        cols = pl.ds(pl.multiple_of(i * chunk, chunk), chunk)
        s = lax.dot_general(
            q, c_ref[cols, :], (((1,), (1,)), ((), ())), preferred_element_type=jnp.float32
        ) * beta
        s_sc[:, cols] = s
        m = m_sc[...]
        for j in range(chunk // lanes):
            m = jnp.maximum(m, s[:, j * lanes:(j + 1) * lanes])
        m_sc[...] = m

    top = jnp.max(m_sc[...], axis=1, keepdims=True)
    l_sc[...] = jnp.zeros(l_sc.shape, jnp.float32)
    acc_sc[...] = jnp.zeros(acc_sc.shape, jnp.float32)

    @pl.loop(0, n_chunks)
    def _(i):
        cols = pl.ds(pl.multiple_of(i * chunk, chunk), chunk)
        w = jnp.exp(s_sc[:, cols] - top).astype(jnp.bfloat16)
        wf = w.astype(jnp.float32)
        l = l_sc[...]
        for j in range(chunk // lanes):
            l = l + wf[:, j * lanes:(j + 1) * lanes]
        l_sc[...] = l
        acc_sc[...] += jnp.dot(w, c_ref[cols, :], preferred_element_type=jnp.float32)

    total = jnp.sum(l_sc[...], axis=1, keepdims=True)
    o_ref[...] = (acc_sc[...] / total).astype(o_ref.dtype)


def soft_reconstruct(queries, cents):
    slots, width = queries.shape
    n_cent = cents.shape[0]
    chunk = min(2048, n_cent)
    tq = min(512, slots, (16 << 20) // (4 * n_cent))
    vmem = 4 * tq * n_cent + 2 * 2 * n_cent * width + 8 * tq * width * 4 + (8 << 20)
    return pl.pallas_call(
        functools.partial(_soft_kernel, chunk=chunk, beta=1.0 / math.sqrt(width)),
        out_shape=jax.ShapeDtypeStruct((slots, width), jnp.bfloat16),
        grid=(slots // tq,),
        in_specs=[
            pl.BlockSpec((tq, width), lambda i: (i, 0)),
            pl.BlockSpec((n_cent, width), lambda i: (0, 0)),
        ],
        out_specs=pl.BlockSpec((tq, width), lambda i: (i, 0)),
        scratch_shapes=[
            pltpu.VMEM((tq, 128), jnp.float32),
            pltpu.VMEM((tq, 128), jnp.float32),
            pltpu.VMEM((tq, width), jnp.float32),
            pltpu.VMEM((tq, n_cent), jnp.float32),
        ],
        compiler_params=pltpu.CompilerParams(vmem_limit_bytes=min(vmem, 60 << 20)),
        cost_estimate=pl.CostEstimate(
            flops=2 * 2 * slots * n_cent * width,
            transcendentals=slots * n_cent,
            bytes_accessed=2 * (2 * slots * width + n_cent * width),
        ),
    )(queries, cents)


def _shift(x, axis, n, d):
    return lax.ppermute(x, axis, [(i, (i + d) % n) for i in range(n)])


def _gather_partition(centroids):
    n_blk = lax.axis_size("blk")
    n_chip = n_blk // 2
    chip = lax.axis_index("blk") // 2

    def over_chips(x, moves):
        return lax.ppermute(x, "blk", [(k * 2 + c, j * 2 + c) for k, j in moves for c in range(2)])

    if n_chip == 4:
        up = over_chips(centroids, [(0, 1), (1, 2), (2, 3)])
        down = over_chips(centroids, [(1, 0), (2, 1), (3, 2)])
        two = over_chips(centroids, [(0, 2), (1, 3), (2, 0), (3, 1)])
        relay = over_chips(two, [(2, 3), (1, 0)])
        pieces = [centroids, jnp.where(chip == 0, relay, up), jnp.where(chip == 3, relay, down), two]
    else:
        pieces = [centroids] + [
            over_chips(centroids, [(k, (k + d) % n_chip) for k in range(n_chip)])
            for d in range(1, n_chip)
        ]
    swap = [(b, b ^ 1) for b in range(n_blk)]
    swapped = [lax.ppermute(p, "blk", swap) for p in pieces]
    return jnp.concatenate(pieces + swapped, axis=0)


def local(codes, scales, coarse_ids, centroids):
    rows_dev = codes.shape[0]
    width = codes.shape[1]
    loops = lax.axis_size("cell")
    cap = 2 * rows_dev // loops
    me = lax.axis_index("cell")
    dequant = (codes.astype(jnp.float32) * scales[:, None]).astype(jnp.bfloat16)
    onehot = (coarse_ids[:, None] == jnp.arange(loops, dtype=jnp.int32)[None, :]).astype(jnp.int32)
    ranks = jnp.sum(jnp.cumsum(onehot, axis=0) * onehot, axis=1) - 1
    slots = ((coarse_ids - me) % loops) * cap + ranks
    outgoing = jnp.zeros((loops * cap, width), jnp.bfloat16).at[slots].set(dequant)
    outgoing = outgoing.reshape(loops, cap, width)
    part = _gather_partition(centroids)
    arrived = [outgoing[0]] + [_shift(outgoing[d], "cell", loops, d) for d in range(1, loops)]
    queries = jnp.concatenate(arrived, axis=0)
    recon = soft_reconstruct(queries, part).reshape(loops, cap, width)
    back = [recon[0]] + [_shift(recon[d], "cell", loops, -d) for d in range(1, loops)]
    mine = jnp.concatenate(back, axis=0)[slots]
    residual = (dequant.astype(jnp.float32) - mine.astype(jnp.float32)).astype(jnp.bfloat16)
    return (mine, residual)


def solution(mesh):
    rows = P(("cell", "blk"), None)
    in_specs = (rows, P(("cell", "blk")), P(("cell", "blk")), rows)
    out_specs = (rows, rows)
    return jax.shard_map(local, mesh=mesh, in_specs=in_specs, out_specs=out_specs, check_vma=False)
```

```python
import functools
import math

import jax
import jax.numpy as jnp
from jax import lax
from jax.experimental import pallas as pl
from jax.experimental.pallas import tpu as pltpu
from jax.sharding import PartitionSpec as P


def _soft_kernel(q_ref, c_ref, o_ref, m_sc, l_sc, acc_sc, s_sc, *, chunk, beta):
    n_chunks = c_ref.shape[0] // chunk
    lanes = m_sc.shape[1]
    q = q_ref[...]
    m_sc[...] = jnp.full(m_sc.shape, -jnp.inf, jnp.float32)

    @pl.loop(0, n_chunks)
    def _(i):
        cols = pl.ds(pl.multiple_of(i * chunk, chunk), chunk)
        s = lax.dot_general(
            q, c_ref[cols, :], (((1,), (1,)), ((), ())), preferred_element_type=jnp.float32
        ) * beta
        s_sc[:, cols] = s
        m = m_sc[...]
        for j in range(chunk // lanes):
            m = jnp.maximum(m, s[:, j * lanes:(j + 1) * lanes])
        m_sc[...] = m

    top = jnp.max(m_sc[...], axis=1, keepdims=True)
    l_sc[...] = jnp.zeros(l_sc.shape, jnp.float32)
    acc_sc[...] = jnp.zeros(acc_sc.shape, jnp.float32)

    @pl.loop(0, n_chunks)
    def _(i):
        cols = pl.ds(pl.multiple_of(i * chunk, chunk), chunk)
        w = jnp.exp(s_sc[:, cols] - top).astype(jnp.bfloat16)
        wf = w.astype(jnp.float32)
        l = l_sc[...]
        for j in range(chunk // lanes):
            l = l + wf[:, j * lanes:(j + 1) * lanes]
        l_sc[...] = l
        acc_sc[...] += jnp.dot(w, c_ref[cols, :], preferred_element_type=jnp.float32)

    total = jnp.sum(l_sc[...], axis=1, keepdims=True)
    o_ref[...] = (acc_sc[...] / total).astype(o_ref.dtype)


def soft_reconstruct(queries, cents):
    slots, width = queries.shape
    n_cent = cents.shape[0]
    chunk = min(4096, n_cent)
    tq = min(512, slots, (32 << 20) // (4 * n_cent))
    vmem = 4 * tq * n_cent + 2 * 2 * n_cent * width + 8 * tq * width * 4 + (8 << 20)
    return pl.pallas_call(
        functools.partial(_soft_kernel, chunk=chunk, beta=1.0 / math.sqrt(width)),
        out_shape=jax.ShapeDtypeStruct((slots, width), jnp.bfloat16),
        grid=(slots // tq,),
        in_specs=[
            pl.BlockSpec((tq, width), lambda i: (i, 0)),
            pl.BlockSpec((n_cent, width), lambda i: (0, 0)),
        ],
        out_specs=pl.BlockSpec((tq, width), lambda i: (i, 0)),
        scratch_shapes=[
            pltpu.VMEM((tq, 128), jnp.float32),
            pltpu.VMEM((tq, 128), jnp.float32),
            pltpu.VMEM((tq, width), jnp.float32),
            pltpu.VMEM((tq, n_cent), jnp.float32),
        ],
        compiler_params=pltpu.CompilerParams(vmem_limit_bytes=min(vmem, 60 << 20)),
        cost_estimate=pl.CostEstimate(
            flops=2 * 2 * slots * n_cent * width,
            transcendentals=slots * n_cent,
            bytes_accessed=2 * (2 * slots * width + n_cent * width),
        ),
    )(queries, cents)


def _shift(x, axis, n, d):
    return lax.ppermute(x, axis, [(i, (i + d) % n) for i in range(n)])


def _gather_partition(centroids):
    n_blk = lax.axis_size("blk")
    n_chip = n_blk // 2
    chip = lax.axis_index("blk") // 2

    def over_chips(x, moves):
        return lax.ppermute(x, "blk", [(k * 2 + c, j * 2 + c) for k, j in moves for c in range(2)])

    if n_chip == 4:
        up = over_chips(centroids, [(0, 1), (1, 2), (2, 3)])
        down = over_chips(centroids, [(1, 0), (2, 1), (3, 2)])
        two = over_chips(centroids, [(0, 2), (1, 3), (2, 0), (3, 1)])
        relay = over_chips(two, [(2, 3), (1, 0)])
        pieces = [centroids, jnp.where(chip == 0, relay, up), jnp.where(chip == 3, relay, down), two]
    else:
        pieces = [centroids] + [
            over_chips(centroids, [(k, (k + d) % n_chip) for k in range(n_chip)])
            for d in range(1, n_chip)
        ]
    swap = [(b, b ^ 1) for b in range(n_blk)]
    swapped = [lax.ppermute(p, "blk", swap) for p in pieces]
    return jnp.concatenate(pieces + swapped, axis=0)


def local(codes, scales, coarse_ids, centroids):
    rows_dev = codes.shape[0]
    width = codes.shape[1]
    loops = lax.axis_size("cell")
    cap = 2 * rows_dev // loops
    me = lax.axis_index("cell")
    dequant = (codes.astype(jnp.float32) * scales[:, None]).astype(jnp.bfloat16)
    onehot = (coarse_ids[:, None] == jnp.arange(loops, dtype=jnp.int32)[None, :]).astype(jnp.int32)
    ranks = jnp.sum(jnp.cumsum(onehot, axis=0) * onehot, axis=1) - 1
    slots = ((coarse_ids - me) % loops) * cap + ranks
    outgoing = jnp.zeros((loops * cap, width), jnp.bfloat16).at[slots].set(dequant)
    outgoing = outgoing.reshape(loops, cap, width)
    part = _gather_partition(centroids)
    arrived = [outgoing[0]] + [_shift(outgoing[d], "cell", loops, d) for d in range(1, loops)]
    half = loops // 2
    first = soft_reconstruct(jnp.concatenate(arrived[1:half + 1], axis=0), part)
    rest = arrived[half + 1:] + arrived[:1]
    second = soft_reconstruct(jnp.concatenate(rest, axis=0), part)
    done = list(first.reshape(half, cap, width)) + list(second.reshape(loops - half, cap, width))
    order = list(range(1, loops)) + [0]
    recon = dict(zip(order, done))
    back = [recon[0]] + [_shift(recon[d], "cell", loops, -d) for d in range(1, loops)]
    mine = jnp.concatenate(back, axis=0)[slots]
    residual = (dequant.astype(jnp.float32) - mine.astype(jnp.float32)).astype(jnp.bfloat16)
    return (mine, residual)


def solution(mesh):
    rows = P(("cell", "blk"), None)
    in_specs = (rows, P(("cell", "blk")), P(("cell", "blk")), rows)
    out_specs = (rows, rows)
    return jax.shard_map(local, mesh=mesh, in_specs=in_specs, out_specs=out_specs, check_vma=False)
```

```python
import functools
import math

import jax
import jax.numpy as jnp
from jax import lax
from jax.experimental import pallas as pl
from jax.experimental.pallas import tpu as pltpu
from jax.sharding import PartitionSpec as P


def _soft_kernel(*refs, chunk, beta, merge):
    if merge:
        q_ref, c_ref, pm_ref, pl_ref, pacc_ref, o_ref, m_sc, l_sc, acc_sc, s_sc = refs
    else:
        q_ref, c_ref, om_ref, ol_ref, oacc_ref, m_sc, l_sc, acc_sc, s_sc = refs
    n_chunks = c_ref.shape[0] // chunk
    lanes = m_sc.shape[1]
    q = q_ref[...]
    m_sc[...] = jnp.full(m_sc.shape, -jnp.inf, jnp.float32)

    @pl.loop(0, n_chunks)
    def _(i):
        cols = pl.ds(pl.multiple_of(i * chunk, chunk), chunk)
        s = lax.dot_general(
            q, c_ref[cols, :], (((1,), (1,)), ((), ())), preferred_element_type=jnp.float32
        ) * beta
        s_sc[:, cols] = s
        m = m_sc[...]
        for j in range(chunk // lanes):
            m = jnp.maximum(m, s[:, j * lanes:(j + 1) * lanes])
        m_sc[...] = m

    top = jnp.max(m_sc[...], axis=1, keepdims=True)
    if merge:
        top = jnp.maximum(top, pm_ref[...])
    l_sc[...] = jnp.zeros(l_sc.shape, jnp.float32)
    acc_sc[...] = jnp.zeros(acc_sc.shape, jnp.float32)

    @pl.loop(0, n_chunks)
    def _(i):
        cols = pl.ds(pl.multiple_of(i * chunk, chunk), chunk)
        w = jnp.exp(s_sc[:, cols] - top).astype(jnp.bfloat16)
        wf = w.astype(jnp.float32)
        l = l_sc[...]
        for j in range(chunk // lanes):
            l = l + wf[:, j * lanes:(j + 1) * lanes]
        l_sc[...] = l
        acc_sc[...] += jnp.dot(w, c_ref[cols, :], preferred_element_type=jnp.float32)

    total = jnp.sum(l_sc[...], axis=1, keepdims=True)
    if merge:
        scale = jnp.exp(pm_ref[...] - top)
        total = total + pl_ref[...] * scale
        numer = acc_sc[...] + pacc_ref[...] * scale
        o_ref[...] = (numer / total).astype(o_ref.dtype)
    else:
        om_ref[...] = top
        ol_ref[...] = total
        oacc_ref[...] = acc_sc[...]


def soft_part(queries, cents, prior=None):
    slots, width = queries.shape
    n_cent = cents.shape[0]
    chunk = min(4096, n_cent)
    tq = min(1024, slots, (32 << 20) // (4 * n_cent))
    vmem = 4 * tq * n_cent + 2 * 2 * n_cent * width + 16 * tq * width * 4 + (8 << 20)
    rows = pl.BlockSpec((tq, width), lambda i: (i, 0))
    col = pl.BlockSpec((tq, 1), lambda i: (i, 0))
    in_specs = [rows, pl.BlockSpec((n_cent, width), lambda i: (0, 0))]
    stats = [
        jax.ShapeDtypeStruct((slots, 1), jnp.float32),
        jax.ShapeDtypeStruct((slots, 1), jnp.float32),
        jax.ShapeDtypeStruct((slots, width), jnp.float32),
    ]
    if prior is None:
        out_shape, out_specs, args = stats, [col, col, rows], (queries, cents)
    else:
        in_specs += [col, col, rows]
        out_shape = jax.ShapeDtypeStruct((slots, width), jnp.bfloat16)
        out_specs, args = rows, (queries, cents) + tuple(prior)
    return pl.pallas_call(
        functools.partial(
            _soft_kernel, chunk=chunk, beta=1.0 / math.sqrt(width), merge=prior is not None
        ),
        out_shape=out_shape,
        grid=(slots // tq,),
        in_specs=in_specs,
        out_specs=out_specs,
        scratch_shapes=[
            pltpu.VMEM((tq, 128), jnp.float32),
            pltpu.VMEM((tq, 128), jnp.float32),
            pltpu.VMEM((tq, width), jnp.float32),
            pltpu.VMEM((tq, n_cent), jnp.float32),
        ],
        compiler_params=pltpu.CompilerParams(vmem_limit_bytes=min(vmem, 60 << 20)),
        cost_estimate=pl.CostEstimate(
            flops=2 * 2 * slots * n_cent * width,
            transcendentals=slots * n_cent,
            bytes_accessed=2 * (2 * slots * width + n_cent * width),
        ),
    )(*args)


def _shift(x, axis, n, d):
    return lax.ppermute(x, axis, [(i, (i + d) % n) for i in range(n)])


def _gather_partition(centroids):
    n_blk = lax.axis_size("blk")
    n_chip = n_blk // 2
    chip = lax.axis_index("blk") // 2

    def over_chips(x, moves):
        return lax.ppermute(x, "blk", [(k * 2 + c, j * 2 + c) for k, j in moves for c in range(2)])

    if n_chip == 4:
        up = over_chips(centroids, [(0, 1), (1, 2), (2, 3)])
        down = over_chips(centroids, [(1, 0), (2, 1), (3, 2)])
        two = over_chips(centroids, [(0, 2), (1, 3), (2, 0), (3, 1)])
        relay = over_chips(two, [(2, 3), (1, 0)])
        pieces = [centroids, two, jnp.where(chip == 0, relay, up), jnp.where(chip == 3, relay, down)]
    else:
        pieces = [centroids] + [
            over_chips(centroids, [(k, (k + d) % n_chip) for k in range(n_chip)])
            for d in range(1, n_chip)
        ]
    swap = [(b, b ^ 1) for b in range(n_blk)]
    swapped = [lax.ppermute(p, "blk", swap) for p in pieces]
    k = len(pieces) // 2
    early = jnp.concatenate(pieces[:k] + swapped[:k], axis=0)
    late = jnp.concatenate(pieces[k:] + swapped[k:], axis=0)
    return early, late


def _local(codes, scales, coarse_ids, centroids):
    rows_dev = codes.shape[0]
    width = codes.shape[1]
    loops = lax.axis_size("cell")
    cap = 2 * rows_dev // loops
    me = lax.axis_index("cell")
    dequant = (codes.astype(jnp.float32) * scales[:, None]).astype(jnp.bfloat16)
    onehot = (coarse_ids[:, None] == jnp.arange(loops, dtype=jnp.int32)[None, :]).astype(jnp.int32)
    ranks = jnp.sum(jnp.cumsum(onehot, axis=0) * onehot, axis=1) - 1
    slots = ((coarse_ids - me) % loops) * cap + ranks
    outgoing = jnp.zeros((loops * cap, width), jnp.bfloat16).at[slots].set(dequant)
    outgoing = outgoing.reshape(loops, cap, width)
    early, late = _gather_partition(centroids)
    arrived = [outgoing[0]] + [_shift(outgoing[d], "cell", loops, d) for d in range(1, loops)]
    queries = jnp.concatenate(arrived, axis=0)
    prior = soft_part(queries, early)
    recon = soft_part(queries, late, prior).reshape(loops, cap, width)
    back = [recon[0]] + [_shift(recon[d], "cell", loops, -d) for d in range(1, loops)]
    mine = jnp.concatenate(back, axis=0)[slots]
    residual = (dequant.astype(jnp.float32) - mine.astype(jnp.float32)).astype(jnp.bfloat16)
    return (mine, residual)


def solution(mesh):
    rows = P(("cell", "blk"), None)
    in_specs = (rows, P(("cell", "blk")), P(("cell", "blk")), rows)
    out_specs = (rows, rows)
    return jax.shard_map(_local, mesh=mesh, in_specs=in_specs, out_specs=out_specs, check_vma=False)
```

```python
import functools
import math

import jax
import jax.numpy as jnp
from jax import lax
from jax.experimental import pallas as pl
from jax.experimental.pallas import tpu as pltpu
from jax.sharding import PartitionSpec as P


def _soft_kernel(*refs, chunk, beta, merge, final):
    if not merge and final:
        q_ref, c_ref, o_ref, m_sc, l_sc, acc_sc, s_sc = refs
    elif merge:
        q_ref, c_ref, pm_ref, pl_ref, pacc_ref, o_ref, m_sc, l_sc, acc_sc, s_sc = refs
    else:
        q_ref, c_ref, om_ref, ol_ref, oacc_ref, m_sc, l_sc, acc_sc, s_sc = refs
    n_chunks = c_ref.shape[0] // chunk
    lanes = m_sc.shape[1]
    q = q_ref[...]
    m_sc[...] = jnp.full(m_sc.shape, -jnp.inf, jnp.float32)

    @pl.loop(0, n_chunks)
    def _(i):
        cols = pl.ds(pl.multiple_of(i * chunk, chunk), chunk)
        s = lax.dot_general(
            q, c_ref[cols, :], (((1,), (1,)), ((), ())), preferred_element_type=jnp.float32
        ) * beta
        s_sc[:, cols] = s
        m = m_sc[...]
        for j in range(chunk // lanes):
            m = jnp.maximum(m, s[:, j * lanes:(j + 1) * lanes])
        m_sc[...] = m

    top = jnp.max(m_sc[...], axis=1, keepdims=True)
    if merge:
        top = jnp.maximum(top, pm_ref[...])
    l_sc[...] = jnp.zeros(l_sc.shape, jnp.float32)
    acc_sc[...] = jnp.zeros(acc_sc.shape, jnp.float32)

    @pl.loop(0, n_chunks)
    def _(i):
        cols = pl.ds(pl.multiple_of(i * chunk, chunk), chunk)
        w = jnp.exp(s_sc[:, cols] - top).astype(jnp.bfloat16)
        wf = w.astype(jnp.float32)
        l = l_sc[...]
        for j in range(chunk // lanes):
            l = l + wf[:, j * lanes:(j + 1) * lanes]
        l_sc[...] = l
        acc_sc[...] += jnp.dot(w, c_ref[cols, :], preferred_element_type=jnp.float32)

    total = jnp.sum(l_sc[...], axis=1, keepdims=True)
    if final and not merge:
        o_ref[...] = (acc_sc[...] / total).astype(o_ref.dtype)
    elif merge:
        scale = jnp.exp(pm_ref[...] - top)
        total = total + pl_ref[...] * scale
        numer = acc_sc[...] + pacc_ref[...] * scale
        o_ref[...] = (numer / total).astype(o_ref.dtype)
    else:
        om_ref[...] = top
        ol_ref[...] = total
        oacc_ref[...] = acc_sc[...]


def soft_part(queries, cents, prior=None, final=False):
    slots, width = queries.shape
    n_cent = cents.shape[0]
    chunk = min(4096, n_cent)
    tq = min(1024, slots, (32 << 20) // (4 * n_cent))
    vmem = 4 * tq * n_cent + 2 * 2 * n_cent * width + 16 * tq * width * 4 + (8 << 20)
    rows = pl.BlockSpec((tq, width), lambda i: (i, 0))
    col = pl.BlockSpec((tq, 1), lambda i: (i, 0))
    in_specs = [rows, pl.BlockSpec((n_cent, width), lambda i: (0, 0))]
    stats = [
        jax.ShapeDtypeStruct((slots, 1), jnp.float32),
        jax.ShapeDtypeStruct((slots, 1), jnp.float32),
        jax.ShapeDtypeStruct((slots, width), jnp.float32),
    ]
    if prior is None and final:
        out_shape = jax.ShapeDtypeStruct((slots, width), jnp.bfloat16)
        out_specs, args = rows, (queries, cents)
    elif prior is None:
        out_shape, out_specs, args = stats, [col, col, rows], (queries, cents)
    else:
        in_specs += [col, col, rows]
        out_shape = jax.ShapeDtypeStruct((slots, width), jnp.bfloat16)
        out_specs, args = rows, (queries, cents) + tuple(prior)
    return pl.pallas_call(
        functools.partial(
            _soft_kernel,
            chunk=chunk,
            beta=1.0 / math.sqrt(width),
            merge=prior is not None,
            final=final or prior is not None,
        ),
        out_shape=out_shape,
        grid=(slots // tq,),
        in_specs=in_specs,
        out_specs=out_specs,
        scratch_shapes=[
            pltpu.VMEM((tq, 128), jnp.float32),
            pltpu.VMEM((tq, 128), jnp.float32),
            pltpu.VMEM((tq, width), jnp.float32),
            pltpu.VMEM((tq, n_cent), jnp.float32),
        ],
        compiler_params=pltpu.CompilerParams(vmem_limit_bytes=min(vmem, 60 << 20)),
        cost_estimate=pl.CostEstimate(
            flops=2 * 2 * slots * n_cent * width,
            transcendentals=slots * n_cent,
            bytes_accessed=2 * (2 * slots * width + n_cent * width),
        ),
    )(*args)


def _shift(x, axis, n, d):
    return lax.ppermute(x, axis, [(i, (i + d) % n) for i in range(n)])


def _gather_partition(centroids):
    n_blk = lax.axis_size("blk")
    n_chip = n_blk // 2
    pieces = [centroids]
    for d in range(1, n_chip):
        pairs = [(k * 2 + c, ((k + d) % n_chip) * 2 + c) for k in range(n_chip) for c in range(2)]
        pieces.append(lax.ppermute(centroids, "blk", pairs))
    swap = [(b, b ^ 1) for b in range(n_blk)]
    swapped = [lax.ppermute(p, "blk", swap) for p in pieces]
    return jnp.concatenate(pieces + swapped, axis=0)


def local(codes, scales, coarse_ids, centroids):
    rows_dev = codes.shape[0]
    width = codes.shape[1]
    loops = lax.axis_size("cell")
    cap = 2 * rows_dev // loops
    me = lax.axis_index("cell")
    dequant = (codes.astype(jnp.float32) * scales[:, None]).astype(jnp.bfloat16)
    onehot = (coarse_ids[:, None] == jnp.arange(loops, dtype=jnp.int32)[None, :]).astype(jnp.int32)
    ranks = jnp.sum(jnp.cumsum(onehot, axis=0) * onehot, axis=1) - 1
    slots = ((coarse_ids - me) % loops) * cap + ranks
    outgoing = jnp.zeros((loops * cap, width), jnp.bfloat16).at[slots].set(dequant)
    outgoing = outgoing.reshape(loops, cap, width)
    part = _gather_partition(centroids)
    arrived = [outgoing[0]] + [_shift(outgoing[d], "cell", loops, d) for d in range(1, loops)]
    queries = jnp.concatenate(arrived, axis=0)
    recon = soft_part(queries, part, final=True).reshape(loops, cap, width)
    back = [recon[0]] + [_shift(recon[d], "cell", loops, -d) for d in range(1, loops)]
    mine = jnp.concatenate(back, axis=0)[slots]
    residual = (dequant.astype(jnp.float32) - mine.astype(jnp.float32)).astype(jnp.bfloat16)
    return (mine, residual)


def solution(mesh):
    rows = P(("cell", "blk"), None)
    in_specs = (rows, P(("cell", "blk")), P(("cell", "blk")), rows)
    out_specs = (rows, rows)
    return jax.shard_map(local, mesh=mesh, in_specs=in_specs, out_specs=out_specs, check_vma=False)
```

```python
import functools
import math

import jax
import jax.numpy as jnp
from jax import lax
from jax.experimental import pallas as pl
from jax.experimental.pallas import tpu as pltpu
from jax.sharding import PartitionSpec as P


def _soft_kernel(*refs, chunk, beta, merge, final):
    if not merge and final:
        q_ref, c_ref, o_ref, m_sc, l_sc, acc_sc, s_sc = refs
    elif merge:
        q_ref, c_ref, pm_ref, pl_ref, pacc_ref, o_ref, m_sc, l_sc, acc_sc, s_sc = refs
    else:
        q_ref, c_ref, om_ref, ol_ref, oacc_ref, m_sc, l_sc, acc_sc, s_sc = refs
    n_chunks = c_ref.shape[0] // chunk
    lanes = m_sc.shape[1]
    q = q_ref[...]
    m_sc[...] = jnp.full(m_sc.shape, -jnp.inf, jnp.float32)

    @pl.loop(0, n_chunks)
    def _(i):
        cols = pl.ds(pl.multiple_of(i * chunk, chunk), chunk)
        s = lax.dot_general(
            q, c_ref[cols, :], (((1,), (1,)), ((), ())), preferred_element_type=jnp.float32
        ) * beta
        s_sc[:, cols] = s
        m = m_sc[...]
        for j in range(chunk // lanes):
            m = jnp.maximum(m, s[:, j * lanes:(j + 1) * lanes])
        m_sc[...] = m

    top = jnp.max(m_sc[...], axis=1, keepdims=True)
    if merge:
        top = jnp.maximum(top, pm_ref[...])
    l_sc[...] = jnp.zeros(l_sc.shape, jnp.float32)
    acc_sc[...] = jnp.zeros(acc_sc.shape, jnp.float32)

    @pl.loop(0, n_chunks)
    def _(i):
        cols = pl.ds(pl.multiple_of(i * chunk, chunk), chunk)
        w = jnp.exp(s_sc[:, cols] - top).astype(jnp.bfloat16)
        wf = w.astype(jnp.float32)
        l = l_sc[...]
        for j in range(chunk // lanes):
            l = l + wf[:, j * lanes:(j + 1) * lanes]
        l_sc[...] = l
        acc_sc[...] += jnp.dot(w, c_ref[cols, :], preferred_element_type=jnp.float32)

    total = jnp.sum(l_sc[...], axis=1, keepdims=True)
    if final and not merge:
        o_ref[...] = (acc_sc[...] / total).astype(o_ref.dtype)
    elif merge:
        scale = jnp.exp(pm_ref[...] - top)
        total = total + pl_ref[...] * scale
        numer = acc_sc[...] + pacc_ref[...] * scale
        o_ref[...] = (numer / total).astype(o_ref.dtype)
    else:
        om_ref[...] = top
        ol_ref[...] = total
        oacc_ref[...] = acc_sc[...]


def soft_part(queries, cents, prior=None, final=False):
    slots, width = queries.shape
    n_cent = cents.shape[0]
    chunk = min(4096, n_cent)
    tq = min(1024, slots, (32 << 20) // (4 * n_cent))
    vmem = 4 * tq * n_cent + 2 * 2 * n_cent * width + 16 * tq * width * 4 + (8 << 20)
    rows = pl.BlockSpec((tq, width), lambda i: (i, 0))
    col = pl.BlockSpec((tq, 1), lambda i: (i, 0))
    in_specs = [rows, pl.BlockSpec((n_cent, width), lambda i: (0, 0))]
    stats = [
        jax.ShapeDtypeStruct((slots, 1), jnp.float32),
        jax.ShapeDtypeStruct((slots, 1), jnp.float32),
        jax.ShapeDtypeStruct((slots, width), jnp.float32),
    ]
    if prior is None and final:
        out_shape = jax.ShapeDtypeStruct((slots, width), jnp.bfloat16)
        out_specs, args = rows, (queries, cents)
    elif prior is None:
        out_shape, out_specs, args = stats, [col, col, rows], (queries, cents)
    else:
        in_specs += [col, col, rows]
        out_shape = jax.ShapeDtypeStruct((slots, width), jnp.bfloat16)
        out_specs, args = rows, (queries, cents) + tuple(prior)
    return pl.pallas_call(
        functools.partial(
            _soft_kernel,
            chunk=chunk,
            beta=1.0 / math.sqrt(width),
            merge=prior is not None,
            final=final or prior is not None,
        ),
        out_shape=out_shape,
        grid=(slots // tq,),
        in_specs=in_specs,
        out_specs=out_specs,
        scratch_shapes=[
            pltpu.VMEM((tq, 128), jnp.float32),
            pltpu.VMEM((tq, 128), jnp.float32),
            pltpu.VMEM((tq, width), jnp.float32),
            pltpu.VMEM((tq, n_cent), jnp.float32),
        ],
        compiler_params=pltpu.CompilerParams(vmem_limit_bytes=min(vmem, 60 << 20)),
        cost_estimate=pl.CostEstimate(
            flops=2 * 2 * slots * n_cent * width,
            transcendentals=slots * n_cent,
            bytes_accessed=2 * (2 * slots * width + n_cent * width),
        ),
    )(*args)


def _shift(x, axis, n, d):
    return lax.ppermute(x, axis, [(i, (i + d) % n) for i in range(n)])


def _gather_partition(centroids):
    n_blk = lax.axis_size("blk")
    n_chip = n_blk // 2
    pieces = [centroids]
    for d in range(1, n_chip):
        pairs = [(k * 2 + c, ((k + d) % n_chip) * 2 + c) for k in range(n_chip) for c in range(2)]
        pieces.append(lax.ppermute(centroids, "blk", pairs))
    swap = [(b, b ^ 1) for b in range(n_blk)]
    swapped = [lax.ppermute(p, "blk", swap) for p in pieces]
    return jnp.concatenate(pieces + swapped, axis=0)


def local(codes, scales, coarse_ids, centroids):
    rows_dev = codes.shape[0]
    width = codes.shape[1]
    loops = lax.axis_size("cell")
    cap = 2 * rows_dev // loops
    me = lax.axis_index("cell")
    dequant = (codes.astype(jnp.float32) * scales[:, None]).astype(jnp.bfloat16)
    onehot = (coarse_ids[:, None] == jnp.arange(loops, dtype=jnp.int32)[None, :]).astype(jnp.int32)
    ranks = jnp.sum(jnp.cumsum(onehot, axis=0) * onehot, axis=1) - 1
    slots = ((coarse_ids - me) % loops) * cap + ranks
    outgoing = jnp.zeros((loops * cap, width), jnp.bfloat16).at[slots].set(dequant)
    outgoing = outgoing.reshape(loops, cap, width)
    part = _gather_partition(centroids)
    arrived = [outgoing[0]] + [_shift(outgoing[d], "cell", loops, d) for d in range(1, loops)]
    half = loops // 2
    first = soft_part(jnp.concatenate(arrived[1:half + 1], axis=0), part, final=True)
    ret = {d: _shift(first[(d - 1) * cap:d * cap], "cell", loops, -d) for d in range(1, half + 1)}
    rest = list(range(half + 1, loops)) + [0]
    second = soft_part(jnp.concatenate([arrived[d] for d in rest], axis=0), part, final=True)
    for i, d in enumerate(rest):
        block = second[i * cap:(i + 1) * cap]
        ret[d] = block if d == 0 else _shift(block, "cell", loops, -d)
    back = [ret[d] for d in range(loops)]
    mine = jnp.concatenate(back, axis=0)[slots]
    residual = (dequant.astype(jnp.float32) - mine.astype(jnp.float32)).astype(jnp.bfloat16)
    return (mine, residual)


def solution(mesh):
    rows = P(("cell", "blk"), None)
    in_specs = (rows, P(("cell", "blk")), P(("cell", "blk")), rows)
    out_specs = (rows, rows)
    return jax.shard_map(local, mesh=mesh, in_specs=in_specs, out_specs=out_specs, check_vma=False)
```

```python
import functools
import math

import jax
import jax.numpy as jnp
from jax import lax
from jax.experimental import pallas as pl
from jax.experimental.pallas import tpu as pltpu
from jax.sharding import PartitionSpec as P


def _soft_kernel(*refs, chunk, beta, merge, final):
    if not merge and final:
        q_ref, c_ref, o_ref, m_sc, l_sc, acc_sc, s_sc = refs
    elif merge:
        q_ref, c_ref, pm_ref, pl_ref, pacc_ref, o_ref, m_sc, l_sc, acc_sc, s_sc = refs
    else:
        q_ref, c_ref, om_ref, ol_ref, oacc_ref, m_sc, l_sc, acc_sc, s_sc = refs
    n_chunks = c_ref.shape[0] // chunk
    lanes = m_sc.shape[1]
    q = q_ref[...]
    m_sc[...] = jnp.full(m_sc.shape, -jnp.inf, jnp.float32)

    @pl.loop(0, n_chunks)
    def _(i):
        cols = pl.ds(pl.multiple_of(i * chunk, chunk), chunk)
        s = lax.dot_general(
            q, c_ref[cols, :], (((1,), (1,)), ((), ())), preferred_element_type=jnp.float32
        ) * beta
        s_sc[:, cols] = s
        m = m_sc[...]
        for j in range(chunk // lanes):
            m = jnp.maximum(m, s[:, j * lanes:(j + 1) * lanes])
        m_sc[...] = m

    top = jnp.max(m_sc[...], axis=1, keepdims=True)
    if merge:
        top = jnp.maximum(top, pm_ref[...])
    l_sc[...] = jnp.zeros(l_sc.shape, jnp.float32)
    acc_sc[...] = jnp.zeros(acc_sc.shape, jnp.float32)

    @pl.loop(0, n_chunks)
    def _(i):
        cols = pl.ds(pl.multiple_of(i * chunk, chunk), chunk)
        w = jnp.exp(s_sc[:, cols] - top).astype(jnp.bfloat16)
        wf = w.astype(jnp.float32)
        l = l_sc[...]
        for j in range(chunk // lanes):
            l = l + wf[:, j * lanes:(j + 1) * lanes]
        l_sc[...] = l
        acc_sc[...] += jnp.dot(w, c_ref[cols, :], preferred_element_type=jnp.float32)

    total = jnp.sum(l_sc[...], axis=1, keepdims=True)
    if final and not merge:
        o_ref[...] = (acc_sc[...] / total).astype(o_ref.dtype)
    elif merge:
        scale = jnp.exp(pm_ref[...] - top)
        total = total + pl_ref[...] * scale
        numer = acc_sc[...] + pacc_ref[...] * scale
        o_ref[...] = (numer / total).astype(o_ref.dtype)
    else:
        om_ref[...] = top
        ol_ref[...] = total
        oacc_ref[...] = acc_sc[...]


def soft_part(queries, cents, prior=None, final=False):
    slots, width = queries.shape
    n_cent = cents.shape[0]
    chunk = min(4096, n_cent)
    tq = min(1024, slots, (32 << 20) // (4 * n_cent))
    vmem = 4 * tq * n_cent + 2 * 2 * n_cent * width + 16 * tq * width * 4 + (8 << 20)
    rows = pl.BlockSpec((tq, width), lambda i: (i, 0))
    col = pl.BlockSpec((tq, 1), lambda i: (i, 0))
    in_specs = [rows, pl.BlockSpec((n_cent, width), lambda i: (0, 0))]
    stats = [
        jax.ShapeDtypeStruct((slots, 1), jnp.float32),
        jax.ShapeDtypeStruct((slots, 1), jnp.float32),
        jax.ShapeDtypeStruct((slots, width), jnp.float32),
    ]
    if prior is None and final:
        out_shape = jax.ShapeDtypeStruct((slots, width), jnp.bfloat16)
        out_specs, args = rows, (queries, cents)
    elif prior is None:
        out_shape, out_specs, args = stats, [col, col, rows], (queries, cents)
    else:
        in_specs += [col, col, rows]
        out_shape = jax.ShapeDtypeStruct((slots, width), jnp.bfloat16)
        out_specs, args = rows, (queries, cents) + tuple(prior)
    return pl.pallas_call(
        functools.partial(
            _soft_kernel,
            chunk=chunk,
            beta=1.0 / math.sqrt(width),
            merge=prior is not None,
            final=final or prior is not None,
        ),
        out_shape=out_shape,
        grid=(slots // tq,),
        in_specs=in_specs,
        out_specs=out_specs,
        scratch_shapes=[
            pltpu.VMEM((tq, 128), jnp.float32),
            pltpu.VMEM((tq, 128), jnp.float32),
            pltpu.VMEM((tq, width), jnp.float32),
            pltpu.VMEM((tq, n_cent), jnp.float32),
        ],
        compiler_params=pltpu.CompilerParams(vmem_limit_bytes=min(vmem, 60 << 20)),
        cost_estimate=pl.CostEstimate(
            flops=2 * 2 * slots * n_cent * width,
            transcendentals=slots * n_cent,
            bytes_accessed=2 * (2 * slots * width + n_cent * width),
        ),
    )(*args)


def _shift(x, axis, n, d):
    return lax.ppermute(x, axis, [(i, (i + d) % n) for i in range(n)])


def _gather_partition(centroids):
    n_blk = lax.axis_size("blk")
    n_chip = n_blk // 2
    pieces = [centroids]
    for d in range(1, n_chip):
        pairs = [(k * 2 + c, ((k + d) % n_chip) * 2 + c) for k in range(n_chip) for c in range(2)]
        pieces.append(lax.ppermute(centroids, "blk", pairs))
    swap = [(b, b ^ 1) for b in range(n_blk)]
    swapped = [lax.ppermute(p, "blk", swap) for p in pieces]
    return jnp.concatenate(pieces + swapped, axis=0)


def _local(codes, scales, coarse_ids, centroids):
    rows_dev = codes.shape[0]
    width = codes.shape[1]
    loops = lax.axis_size("cell")
    cap = 2 * rows_dev // loops
    me = lax.axis_index("cell")
    dequant = (codes.astype(jnp.float32) * scales[:, None]).astype(jnp.bfloat16)
    onehot = (coarse_ids[:, None] == jnp.arange(loops, dtype=jnp.int32)[None, :]).astype(jnp.int32)
    ranks = jnp.sum(jnp.cumsum(onehot, axis=0) * onehot, axis=1) - 1
    slots = ((coarse_ids - me) % loops) * cap + ranks
    outgoing = jnp.zeros((loops * cap, width), jnp.bfloat16).at[slots].set(dequant)
    outgoing = outgoing.reshape(loops, cap, width)
    part = _gather_partition(centroids)
    arrived = [outgoing[0]] + [_shift(outgoing[d], "cell", loops, d) for d in range(1, loops)]
    half = loops // 2
    first = soft_part(jnp.concatenate(arrived[1:half + 1], axis=0), part, final=True)
    ret = {d: _shift(first[(d - 1) * cap:d * cap], "cell", loops, -d) for d in range(1, half + 1)}
    rest = list(range(half + 1, loops)) + [0]
    second = soft_part(jnp.concatenate([arrived[d] for d in rest], axis=0), part, final=True)
    for i, d in enumerate(rest):
        block = second[i * cap:(i + 1) * cap]
        ret[d] = block if d == 0 else _shift(block, "cell", loops, -d)
    last = loops - 1
    rel = slots // cap
    early = [jnp.zeros_like(ret[d]) if d == last else ret[d] for d in range(loops)]
    placed = jnp.concatenate(early, axis=0)[slots]
    pick = (slots[:, None] == last * cap + jnp.arange(cap, dtype=jnp.int32)[None, :]).astype(jnp.bfloat16)
    tail = jnp.dot(pick, ret[last], preferred_element_type=jnp.float32).astype(jnp.bfloat16)
    mine = jnp.where((rel == last)[:, None], tail, placed)
    residual = (dequant.astype(jnp.float32) - mine.astype(jnp.float32)).astype(jnp.bfloat16)
    return (mine, residual)


def solution(mesh):
    rows = P(("cell", "blk"), None)
    in_specs = (rows, P(("cell", "blk")), P(("cell", "blk")), rows)
    out_specs = (rows, rows)
    return jax.shard_map(_local, mesh=mesh, in_specs=in_specs, out_specs=out_specs, check_vma=False)
```

```python
import functools
import math

import jax
import jax.numpy as jnp
from jax import lax
from jax.experimental import pallas as pl
from jax.experimental.pallas import tpu as pltpu
from jax.sharding import PartitionSpec as P


def _soft_kernel(*refs, chunk, beta, merge, final):
    if not merge and final:
        q_ref, c_ref, o_ref, m_sc, l_sc, acc_sc, s_sc = refs
    elif merge:
        q_ref, c_ref, pm_ref, pl_ref, pacc_ref, o_ref, m_sc, l_sc, acc_sc, s_sc = refs
    else:
        q_ref, c_ref, om_ref, ol_ref, oacc_ref, m_sc, l_sc, acc_sc, s_sc = refs
    n_chunks = c_ref.shape[0] // chunk
    lanes = m_sc.shape[1]
    q = q_ref[...]
    m_sc[...] = jnp.full(m_sc.shape, -jnp.inf, jnp.float32)

    @pl.loop(0, n_chunks)
    def _(i):
        cols = pl.ds(pl.multiple_of(i * chunk, chunk), chunk)
        s = lax.dot_general(
            q, c_ref[cols, :], (((1,), (1,)), ((), ())), preferred_element_type=jnp.float32
        ) * beta
        s_sc[:, cols] = s
        m = m_sc[...]
        for j in range(chunk // lanes):
            m = jnp.maximum(m, s[:, j * lanes:(j + 1) * lanes])
        m_sc[...] = m

    top = jnp.max(m_sc[...], axis=1, keepdims=True)
    if merge:
        top = jnp.maximum(top, pm_ref[...])
    l_sc[...] = jnp.zeros(l_sc.shape, jnp.float32)
    acc_sc[...] = jnp.zeros(acc_sc.shape, jnp.float32)

    @pl.loop(0, n_chunks)
    def _(i):
        cols = pl.ds(pl.multiple_of(i * chunk, chunk), chunk)
        w = jnp.exp(s_sc[:, cols] - top).astype(jnp.bfloat16)
        wf = w.astype(jnp.float32)
        l = l_sc[...]
        for j in range(chunk // lanes):
            l = l + wf[:, j * lanes:(j + 1) * lanes]
        l_sc[...] = l
        acc_sc[...] += jnp.dot(w, c_ref[cols, :], preferred_element_type=jnp.float32)

    total = jnp.sum(l_sc[...], axis=1, keepdims=True)
    if final and not merge:
        o_ref[...] = (acc_sc[...] / total).astype(o_ref.dtype)
    elif merge:
        scale = jnp.exp(pm_ref[...] - top)
        total = total + pl_ref[...] * scale
        numer = acc_sc[...] + pacc_ref[...] * scale
        o_ref[...] = (numer / total).astype(o_ref.dtype)
    else:
        om_ref[...] = top
        ol_ref[...] = total
        oacc_ref[...] = acc_sc[...]


def soft_part(queries, cents, prior=None, final=False):
    slots, width = queries.shape
    n_cent = cents.shape[0]
    chunk = min(4096, n_cent)
    tq = slots
    while tq * n_cent * 4 > (32 << 20) and tq % 16 == 0:
        tq //= 2
    vmem = 4 * tq * n_cent + 2 * 2 * n_cent * width + 16 * tq * width * 4 + (8 << 20)
    rows = pl.BlockSpec((tq, width), lambda i: (i, 0))
    col = pl.BlockSpec((tq, 1), lambda i: (i, 0))
    in_specs = [rows, pl.BlockSpec((n_cent, width), lambda i: (0, 0))]
    stats = [
        jax.ShapeDtypeStruct((slots, 1), jnp.float32),
        jax.ShapeDtypeStruct((slots, 1), jnp.float32),
        jax.ShapeDtypeStruct((slots, width), jnp.float32),
    ]
    if prior is None and final:
        out_shape = jax.ShapeDtypeStruct((slots, width), jnp.bfloat16)
        out_specs, args = rows, (queries, cents)
    elif prior is None:
        out_shape, out_specs, args = stats, [col, col, rows], (queries, cents)
    else:
        in_specs += [col, col, rows]
        out_shape = jax.ShapeDtypeStruct((slots, width), jnp.bfloat16)
        out_specs, args = rows, (queries, cents) + tuple(prior)
    return pl.pallas_call(
        functools.partial(
            _soft_kernel,
            chunk=chunk,
            beta=1.0 / math.sqrt(width),
            merge=prior is not None,
            final=final or prior is not None,
        ),
        out_shape=out_shape,
        grid=(slots // tq,),
        in_specs=in_specs,
        out_specs=out_specs,
        scratch_shapes=[
            pltpu.VMEM((tq, 128), jnp.float32),
            pltpu.VMEM((tq, 128), jnp.float32),
            pltpu.VMEM((tq, width), jnp.float32),
            pltpu.VMEM((tq, n_cent), jnp.float32),
        ],
        compiler_params=pltpu.CompilerParams(vmem_limit_bytes=min(vmem, 60 << 20)),
        cost_estimate=pl.CostEstimate(
            flops=2 * 2 * slots * n_cent * width,
            transcendentals=slots * n_cent,
            bytes_accessed=2 * (2 * slots * width + n_cent * width),
        ),
    )(*args)


def _shift(x, axis, n, d):
    return lax.ppermute(x, axis, [(i, (i + d) % n) for i in range(n)])


def _gather_partition(centroids):
    n_blk = lax.axis_size("blk")
    n_chip = n_blk // 2
    pieces = [centroids]
    for d in range(1, n_chip):
        pairs = [(k * 2 + c, ((k + d) % n_chip) * 2 + c) for k in range(n_chip) for c in range(2)]
        pieces.append(lax.ppermute(centroids, "blk", pairs))
    swap = [(b, b ^ 1) for b in range(n_blk)]
    swapped = [lax.ppermute(p, "blk", swap) for p in pieces]
    return jnp.concatenate(pieces + swapped, axis=0)


def _local(codes, scales, coarse_ids, centroids):
    rows_dev = codes.shape[0]
    width = codes.shape[1]
    loops = lax.axis_size("cell")
    cap = 2 * rows_dev // loops
    me = lax.axis_index("cell")
    dequant = (codes.astype(jnp.float32) * scales[:, None]).astype(jnp.bfloat16)
    onehot = (coarse_ids[:, None] == jnp.arange(loops, dtype=jnp.int32)[None, :]).astype(jnp.int32)
    ranks = jnp.sum(jnp.cumsum(onehot, axis=0) * onehot, axis=1) - 1
    slots = ((coarse_ids - me) % loops) * cap + ranks
    outgoing = jnp.zeros((loops * cap, width), jnp.bfloat16).at[slots].set(dequant)
    outgoing = outgoing.reshape(loops, cap, width)
    part = _gather_partition(centroids)
    arrived = [outgoing[0]] + [_shift(outgoing[d], "cell", loops, d) for d in range(1, loops)]
    first = soft_part(jnp.concatenate(arrived[1:], axis=0), part, final=True)
    ret = {d: _shift(first[(d - 1) * cap:d * cap], "cell", loops, -d) for d in range(1, loops)}
    ret[0] = soft_part(arrived[0], part, final=True)
    mine = jnp.concatenate([ret[d] for d in range(loops)], axis=0)[slots]
    residual = (dequant.astype(jnp.float32) - mine.astype(jnp.float32)).astype(jnp.bfloat16)
    return (mine, residual)


def solution(mesh):
    rows = P(("cell", "blk"), None)
    in_specs = (rows, P(("cell", "blk")), P(("cell", "blk")), rows)
    out_specs = (rows, rows)
    return jax.shard_map(_local, mesh=mesh, in_specs=in_specs, out_specs=out_specs, check_vma=False)
```

```python
import functools
import math

import jax
import jax.numpy as jnp
from jax import lax
from jax.experimental import pallas as pl
from jax.experimental.pallas import tpu as pltpu
from jax.sharding import PartitionSpec as P


def _soft_kernel(*refs, chunk, beta, merge, final):
    if not merge and final:
        q_ref, c_ref, o_ref, m_sc, l_sc, acc_sc, s_sc = refs
    elif merge:
        q_ref, c_ref, pm_ref, pl_ref, pacc_ref, o_ref, m_sc, l_sc, acc_sc, s_sc = refs
    else:
        q_ref, c_ref, om_ref, ol_ref, oacc_ref, m_sc, l_sc, acc_sc, s_sc = refs
    n_chunks = c_ref.shape[0] // chunk
    lanes = m_sc.shape[1]
    q = q_ref[...]
    m_sc[...] = jnp.full(m_sc.shape, -jnp.inf, jnp.float32)

    @pl.loop(0, n_chunks)
    def _(i):
        cols = pl.ds(pl.multiple_of(i * chunk, chunk), chunk)
        s = lax.dot_general(
            q, c_ref[cols, :], (((1,), (1,)), ((), ())), preferred_element_type=jnp.float32
        ) * beta
        s_sc[:, cols] = s
        m = m_sc[...]
        for j in range(chunk // lanes):
            m = jnp.maximum(m, s[:, j * lanes:(j + 1) * lanes])
        m_sc[...] = m

    top = jnp.max(m_sc[...], axis=1, keepdims=True)
    if merge:
        top = jnp.maximum(top, pm_ref[...])
    l_sc[...] = jnp.zeros(l_sc.shape, jnp.float32)
    acc_sc[...] = jnp.zeros(acc_sc.shape, jnp.float32)

    @pl.loop(0, n_chunks)
    def _(i):
        cols = pl.ds(pl.multiple_of(i * chunk, chunk), chunk)
        w = jnp.exp(s_sc[:, cols] - top).astype(jnp.bfloat16)
        wf = w.astype(jnp.float32)
        l = l_sc[...]
        for j in range(chunk // lanes):
            l = l + wf[:, j * lanes:(j + 1) * lanes]
        l_sc[...] = l
        acc_sc[...] += jnp.dot(w, c_ref[cols, :], preferred_element_type=jnp.float32)

    total = jnp.sum(l_sc[...], axis=1, keepdims=True)
    if final and not merge:
        o_ref[...] = (acc_sc[...] / total).astype(o_ref.dtype)
    elif merge:
        scale = jnp.exp(pm_ref[...] - top)
        total = total + pl_ref[...] * scale
        numer = acc_sc[...] + pacc_ref[...] * scale
        o_ref[...] = (numer / total).astype(o_ref.dtype)
    else:
        om_ref[...] = top
        ol_ref[...] = total
        oacc_ref[...] = acc_sc[...]


def soft_part(queries, cents, prior=None, final=False):
    slots, width = queries.shape
    n_cent = cents.shape[0]
    chunk = min(4096, n_cent)
    tq = slots
    while tq * n_cent * 4 > (32 << 20) and tq % 16 == 0:
        tq //= 2
    vmem = 4 * tq * n_cent + 2 * 2 * n_cent * width + 16 * tq * width * 4 + (8 << 20)
    rows = pl.BlockSpec((tq, width), lambda i: (i, 0))
    col = pl.BlockSpec((tq, 1), lambda i: (i, 0))
    in_specs = [rows, pl.BlockSpec((n_cent, width), lambda i: (0, 0))]
    stats = [
        jax.ShapeDtypeStruct((slots, 1), jnp.float32),
        jax.ShapeDtypeStruct((slots, 1), jnp.float32),
        jax.ShapeDtypeStruct((slots, width), jnp.float32),
    ]
    if prior is None and final:
        out_shape = jax.ShapeDtypeStruct((slots, width), jnp.bfloat16)
        out_specs, args = rows, (queries, cents)
    elif prior is None:
        out_shape, out_specs, args = stats, [col, col, rows], (queries, cents)
    else:
        in_specs += [col, col, rows]
        out_shape = jax.ShapeDtypeStruct((slots, width), jnp.bfloat16)
        out_specs, args = rows, (queries, cents) + tuple(prior)
    return pl.pallas_call(
        functools.partial(
            _soft_kernel,
            chunk=chunk,
            beta=1.0 / math.sqrt(width),
            merge=prior is not None,
            final=final or prior is not None,
        ),
        out_shape=out_shape,
        grid=(slots // tq,),
        in_specs=in_specs,
        out_specs=out_specs,
        scratch_shapes=[
            pltpu.VMEM((tq, 128), jnp.float32),
            pltpu.VMEM((tq, 128), jnp.float32),
            pltpu.VMEM((tq, width), jnp.float32),
            pltpu.VMEM((tq, n_cent), jnp.float32),
        ],
        compiler_params=pltpu.CompilerParams(vmem_limit_bytes=min(vmem, 60 << 20)),
        cost_estimate=pl.CostEstimate(
            flops=2 * 2 * slots * n_cent * width,
            transcendentals=slots * n_cent,
            bytes_accessed=2 * (2 * slots * width + n_cent * width),
        ),
    )(*args)


def _shift(x, axis, n, d):
    return lax.ppermute(x, axis, [(i, (i + d) % n) for i in range(n)])


def _gather_partition(centroids):
    n_blk = lax.axis_size("blk")
    n_chip = n_blk // 2
    pieces = [centroids]
    for d in range(1, n_chip):
        pairs = [(k * 2 + c, ((k + d) % n_chip) * 2 + c) for k in range(n_chip) for c in range(2)]
        pieces.append(lax.ppermute(centroids, "blk", pairs))
    swap = [(b, b ^ 1) for b in range(n_blk)]
    swapped = [lax.ppermute(p, "blk", swap) for p in pieces]
    return jnp.concatenate(pieces + swapped, axis=0)


def _local(codes, scales, coarse_ids, centroids):
    rows_dev = codes.shape[0]
    width = codes.shape[1]
    loops = lax.axis_size("cell")
    cap = 2 * rows_dev // loops
    me = lax.axis_index("cell")
    dequant = (codes.astype(jnp.float32) * scales[:, None]).astype(jnp.bfloat16)
    onehot = (coarse_ids[:, None] == jnp.arange(loops, dtype=jnp.int32)[None, :]).astype(jnp.int32)
    ranks = jnp.sum(jnp.cumsum(onehot, axis=0) * onehot, axis=1) - 1
    slots = ((coarse_ids - me) % loops) * cap + ranks
    outgoing = jnp.zeros((loops * cap, width), jnp.bfloat16).at[slots].set(dequant)
    outgoing = outgoing.reshape(loops, cap, width)
    part = _gather_partition(centroids)
    arrived = [outgoing[0]] + [_shift(outgoing[d], "cell", loops, d) for d in range(1, loops)]
    first = soft_part(jnp.concatenate(arrived[1:], axis=0), part, final=True)
    ret = {d: _shift(first[(d - 1) * cap:d * cap], "cell", loops, -d) for d in range(1, loops)}
    ret[0] = soft_part(arrived[0], part, final=True)
    rel = slots // cap
    own = ret[0][slots % cap]
    remote = jnp.concatenate([ret[d] for d in range(1, loops)], axis=0)
    pick = (slots[:, None] - cap == jnp.arange(remote.shape[0], dtype=jnp.int32)[None, :])
    tail = jnp.dot(pick.astype(jnp.bfloat16), remote, preferred_element_type=jnp.float32)
    mine = jnp.where((rel == 0)[:, None], own, tail.astype(jnp.bfloat16))
    residual = (dequant.astype(jnp.float32) - mine.astype(jnp.float32)).astype(jnp.bfloat16)
    return (mine, residual)


def solution(mesh):
    rows = P(("cell", "blk"), None)
    in_specs = (rows, P(("cell", "blk")), P(("cell", "blk")), rows)
    out_specs = (rows, rows)
    return jax.shard_map(_local, mesh=mesh, in_specs=in_specs, out_specs=out_specs, check_vma=False)
```

```python
import functools
import math

import jax
import jax.numpy as jnp
from jax import lax
from jax.experimental import pallas as pl
from jax.experimental.pallas import tpu as pltpu
from jax.sharding import PartitionSpec as P


def _soft_kernel(*refs, chunk, beta, merge, final):
    if not merge and final:
        q_ref, c_ref, o_ref, m_sc, l_sc, acc_sc, s_sc = refs
    elif merge:
        q_ref, c_ref, pm_ref, pl_ref, pacc_ref, o_ref, m_sc, l_sc, acc_sc, s_sc = refs
    else:
        q_ref, c_ref, om_ref, ol_ref, oacc_ref, m_sc, l_sc, acc_sc, s_sc = refs
    n_chunks = c_ref.shape[0] // chunk
    lanes = m_sc.shape[1]
    q = q_ref[...]
    m_sc[...] = jnp.full(m_sc.shape, -jnp.inf, jnp.float32)

    @pl.loop(0, n_chunks)
    def _(i):
        cols = pl.ds(pl.multiple_of(i * chunk, chunk), chunk)
        s = lax.dot_general(
            q, c_ref[cols, :], (((1,), (1,)), ((), ())), preferred_element_type=jnp.float32
        ) * beta
        s_sc[:, cols] = s
        m = m_sc[...]
        for j in range(chunk // lanes):
            m = jnp.maximum(m, s[:, j * lanes:(j + 1) * lanes])
        m_sc[...] = m

    top = jnp.max(m_sc[...], axis=1, keepdims=True)
    if merge:
        top = jnp.maximum(top, pm_ref[...])
    l_sc[...] = jnp.zeros(l_sc.shape, jnp.float32)
    acc_sc[...] = jnp.zeros(acc_sc.shape, jnp.float32)

    @pl.loop(0, n_chunks)
    def _(i):
        cols = pl.ds(pl.multiple_of(i * chunk, chunk), chunk)
        w = jnp.exp(s_sc[:, cols] - top).astype(jnp.bfloat16)
        wf = w.astype(jnp.float32)
        l = l_sc[...]
        for j in range(chunk // lanes):
            l = l + wf[:, j * lanes:(j + 1) * lanes]
        l_sc[...] = l
        acc_sc[...] += jnp.dot(w, c_ref[cols, :], preferred_element_type=jnp.float32)

    total = jnp.sum(l_sc[...], axis=1, keepdims=True)
    if final and not merge:
        o_ref[...] = (acc_sc[...] / total).astype(o_ref.dtype)
    elif merge:
        scale = jnp.exp(pm_ref[...] - top)
        total = total + pl_ref[...] * scale
        numer = acc_sc[...] + pacc_ref[...] * scale
        o_ref[...] = (numer / total).astype(o_ref.dtype)
    else:
        om_ref[...] = top
        ol_ref[...] = total
        oacc_ref[...] = acc_sc[...]


def soft_part(queries, cents, prior=None, final=False):
    slots, width = queries.shape
    n_cent = cents.shape[0]
    chunk = min(4096, n_cent)
    tq = slots
    while tq * n_cent * 4 > (32 << 20) and tq % 16 == 0:
        tq //= 2
    vmem = 4 * tq * n_cent + 2 * 2 * n_cent * width + 16 * tq * width * 4 + (8 << 20)
    rows = pl.BlockSpec((tq, width), lambda i: (i, 0))
    col = pl.BlockSpec((tq, 1), lambda i: (i, 0))
    in_specs = [rows, pl.BlockSpec((n_cent, width), lambda i: (0, 0))]
    stats = [
        jax.ShapeDtypeStruct((slots, 1), jnp.float32),
        jax.ShapeDtypeStruct((slots, 1), jnp.float32),
        jax.ShapeDtypeStruct((slots, width), jnp.float32),
    ]
    if prior is None and final:
        out_shape = jax.ShapeDtypeStruct((slots, width), jnp.bfloat16)
        out_specs, args = rows, (queries, cents)
    elif prior is None:
        out_shape, out_specs, args = stats, [col, col, rows], (queries, cents)
    else:
        in_specs += [col, col, rows]
        out_shape = jax.ShapeDtypeStruct((slots, width), jnp.bfloat16)
        out_specs, args = rows, (queries, cents) + tuple(prior)
    return pl.pallas_call(
        functools.partial(
            _soft_kernel,
            chunk=chunk,
            beta=1.0 / math.sqrt(width),
            merge=prior is not None,
            final=final or prior is not None,
        ),
        out_shape=out_shape,
        grid=(slots // tq,),
        in_specs=in_specs,
        out_specs=out_specs,
        scratch_shapes=[
            pltpu.VMEM((tq, 128), jnp.float32),
            pltpu.VMEM((tq, 128), jnp.float32),
            pltpu.VMEM((tq, width), jnp.float32),
            pltpu.VMEM((tq, n_cent), jnp.float32),
        ],
        compiler_params=pltpu.CompilerParams(vmem_limit_bytes=min(vmem, 60 << 20)),
        cost_estimate=pl.CostEstimate(
            flops=2 * 2 * slots * n_cent * width,
            transcendentals=slots * n_cent,
            bytes_accessed=2 * (2 * slots * width + n_cent * width),
        ),
    )(*args)


def _shift(x, axis, n, d):
    return lax.ppermute(x, axis, [(i, (i + d) % n) for i in range(n)])


def _gather_partition(centroids):
    n_blk = lax.axis_size("blk")
    n_chip = n_blk // 2
    chip = lax.axis_index("blk") // 2

    def over_chips(x, moves):
        return lax.ppermute(x, "blk", [(k * 2 + c, j * 2 + c) for k, j in moves for c in range(2)])

    if n_chip == 4:
        up1 = over_chips(centroids, [(0, 1), (1, 2), (2, 3)])
        dn1 = over_chips(centroids, [(1, 0), (2, 1), (3, 2)])
        up2 = over_chips(up1, [(1, 2), (2, 3)])
        dn2 = over_chips(dn1, [(2, 1), (1, 0)])
        up3 = over_chips(up2, [(2, 3)])
        dn3 = over_chips(dn2, [(1, 0)])
        near = jnp.where(chip == 0, dn1, up1)
        mid = jnp.where(chip == 0, dn2, jnp.where(chip == 1, dn1, up2))
        far = jnp.where(chip == 0, dn3, jnp.where(chip == 1, dn2, jnp.where(chip == 2, dn1, up3)))
        pieces = [centroids, near, mid, far]
    else:
        pieces = [centroids]
        for d in range(1, n_chip):
            moves = [(k, (k + d) % n_chip) for k in range(n_chip)]
            pieces.append(over_chips(centroids, moves))
    swap = [(b, b ^ 1) for b in range(n_blk)]
    swapped = [lax.ppermute(p, "blk", swap) for p in pieces]
    return jnp.concatenate(pieces + swapped, axis=0)


def _local(codes, scales, coarse_ids, centroids):
    rows_dev = codes.shape[0]
    width = codes.shape[1]
    loops = lax.axis_size("cell")
    cap = 2 * rows_dev // loops
    me = lax.axis_index("cell")
    dequant = (codes.astype(jnp.float32) * scales[:, None]).astype(jnp.bfloat16)
    onehot = (coarse_ids[:, None] == jnp.arange(loops, dtype=jnp.int32)[None, :]).astype(jnp.int32)
    ranks = jnp.sum(jnp.cumsum(onehot, axis=0) * onehot, axis=1) - 1
    slots = ((coarse_ids - me) % loops) * cap + ranks
    outgoing = jnp.zeros((loops * cap, width), jnp.bfloat16).at[slots].set(dequant)
    outgoing = outgoing.reshape(loops, cap, width)
    part = _gather_partition(centroids)
    arrived = [outgoing[0]] + [_shift(outgoing[d], "cell", loops, d) for d in range(1, loops)]
    first = soft_part(jnp.concatenate(arrived[1:], axis=0), part, final=True)
    ret = {d: _shift(first[(d - 1) * cap:d * cap], "cell", loops, -d) for d in range(1, loops)}
    ret[0] = soft_part(arrived[0], part, final=True)
    back = jnp.concatenate([ret[d] for d in range(loops)], axis=0)
    pick = slots[:, None] == jnp.arange(back.shape[0], dtype=jnp.int32)[None, :]
    mine = jnp.dot(pick.astype(jnp.bfloat16), back, preferred_element_type=jnp.float32)
    mine = mine.astype(jnp.bfloat16)
    residual = (dequant.astype(jnp.float32) - mine.astype(jnp.float32)).astype(jnp.bfloat16)
    return (mine, residual)


def solution(mesh):
    rows = P(("cell", "blk"), None)
    in_specs = (rows, P(("cell", "blk")), P(("cell", "blk")), rows)
    out_specs = (rows, rows)
    return jax.shard_map(_local, mesh=mesh, in_specs=in_specs, out_specs=out_specs, check_vma=False)
```

```python
import functools
import math

import jax
import jax.numpy as jnp
from jax import lax
from jax.experimental import pallas as pl
from jax.experimental.pallas import tpu as pltpu
from jax.sharding import PartitionSpec as P


def _soft_kernel(*refs, chunk, beta, merge, final, counted=False):
    if counted:
        n_ref, refs = refs[0], refs[1:]
        o_ref = refs[2]
        live = pl.program_id(0) * o_ref.shape[0] < n_ref[0]

        @pl.when(live)
        def _():
            _soft_kernel(*refs, chunk=chunk, beta=beta, merge=merge, final=final)

        @pl.when(jnp.logical_not(live))
        def _():
            o_ref[...] = jnp.zeros(o_ref.shape, o_ref.dtype)

        return
    if not merge and final:
        q_ref, c_ref, o_ref, m_sc, l_sc, acc_sc, s_sc = refs
    elif merge:
        q_ref, c_ref, pm_ref, pl_ref, pacc_ref, o_ref, m_sc, l_sc, acc_sc, s_sc = refs
    else:
        q_ref, c_ref, om_ref, ol_ref, oacc_ref, m_sc, l_sc, acc_sc, s_sc = refs
    n_chunks = c_ref.shape[0] // chunk
    lanes = m_sc.shape[1]
    q = q_ref[...]
    m_sc[...] = jnp.full(m_sc.shape, -jnp.inf, jnp.float32)

    @pl.loop(0, n_chunks)
    def _(i):
        cols = pl.ds(pl.multiple_of(i * chunk, chunk), chunk)
        s = lax.dot_general(
            q, c_ref[cols, :], (((1,), (1,)), ((), ())), preferred_element_type=jnp.float32
        ) * beta
        s_sc[:, cols] = s
        m = m_sc[...]
        for j in range(chunk // lanes):
            m = jnp.maximum(m, s[:, j * lanes:(j + 1) * lanes])
        m_sc[...] = m

    top = jnp.max(m_sc[...], axis=1, keepdims=True)
    if merge:
        top = jnp.maximum(top, pm_ref[...])
    l_sc[...] = jnp.zeros(l_sc.shape, jnp.float32)
    acc_sc[...] = jnp.zeros(acc_sc.shape, jnp.float32)

    @pl.loop(0, n_chunks)
    def _(i):
        cols = pl.ds(pl.multiple_of(i * chunk, chunk), chunk)
        w = jnp.exp(s_sc[:, cols] - top).astype(jnp.bfloat16)
        wf = w.astype(jnp.float32)
        l = l_sc[...]
        for j in range(chunk // lanes):
            l = l + wf[:, j * lanes:(j + 1) * lanes]
        l_sc[...] = l
        acc_sc[...] += jnp.dot(w, c_ref[cols, :], preferred_element_type=jnp.float32)

    total = jnp.sum(l_sc[...], axis=1, keepdims=True)
    if final and not merge:
        o_ref[...] = (acc_sc[...] / total).astype(o_ref.dtype)
    elif merge:
        scale = jnp.exp(pm_ref[...] - top)
        total = total + pl_ref[...] * scale
        numer = acc_sc[...] + pacc_ref[...] * scale
        o_ref[...] = (numer / total).astype(o_ref.dtype)
    else:
        om_ref[...] = top
        ol_ref[...] = total
        oacc_ref[...] = acc_sc[...]


def soft_part(queries, cents, prior=None, final=False, count=None, tiles=1):
    slots, width = queries.shape
    n_cent = cents.shape[0]
    chunk = min(4096, n_cent)
    tq = slots // tiles
    while tq * n_cent * 4 > (32 << 20) and tq % 16 == 0:
        tq //= 2
    vmem = 4 * tq * n_cent + 2 * 2 * n_cent * width + 16 * tq * width * 4 + (8 << 20)
    rows = pl.BlockSpec((tq, width), lambda i: (i, 0))
    col = pl.BlockSpec((tq, 1), lambda i: (i, 0))
    in_specs = [rows, pl.BlockSpec((n_cent, width), lambda i: (0, 0))]
    stats = [
        jax.ShapeDtypeStruct((slots, 1), jnp.float32),
        jax.ShapeDtypeStruct((slots, 1), jnp.float32),
        jax.ShapeDtypeStruct((slots, width), jnp.float32),
    ]
    if prior is None and final:
        out_shape = jax.ShapeDtypeStruct((slots, width), jnp.bfloat16)
        out_specs, args = rows, (queries, cents)
    elif prior is None:
        out_shape, out_specs, args = stats, [col, col, rows], (queries, cents)
    else:
        in_specs += [col, col, rows]
        out_shape = jax.ShapeDtypeStruct((slots, width), jnp.bfloat16)
        out_specs, args = rows, (queries, cents) + tuple(prior)
    kernel = functools.partial(
        _soft_kernel,
        chunk=chunk,
        beta=1.0 / math.sqrt(width),
        merge=prior is not None,
        final=final or prior is not None,
        counted=count is not None,
    )
    scratch = [
        pltpu.VMEM((tq, 128), jnp.float32),
        pltpu.VMEM((tq, 128), jnp.float32),
        pltpu.VMEM((tq, width), jnp.float32),
        pltpu.VMEM((tq, n_cent), jnp.float32),
    ]
    params = pltpu.CompilerParams(vmem_limit_bytes=min(vmem, 60 << 20))
    cost = pl.CostEstimate(
        flops=2 * 2 * slots * n_cent * width,
        transcendentals=slots * n_cent,
        bytes_accessed=2 * (2 * slots * width + n_cent * width),
    )
    if count is not None:
        grid_spec = pltpu.PrefetchScalarGridSpec(
            num_scalar_prefetch=1,
            grid=(slots // tq,),
            in_specs=[
                pl.BlockSpec((tq, width), lambda i, n: (i, 0)),
                pl.BlockSpec((n_cent, width), lambda i, n: (0, 0)),
            ],
            out_specs=pl.BlockSpec((tq, width), lambda i, n: (i, 0)),
            scratch_shapes=scratch,
        )
        return pl.pallas_call(
            kernel, out_shape=out_shape, grid_spec=grid_spec, compiler_params=params,
            cost_estimate=cost,
        )(count, *args)
    return pl.pallas_call(
        kernel,
        out_shape=out_shape,
        grid=(slots // tq,),
        in_specs=in_specs,
        out_specs=out_specs,
        scratch_shapes=scratch,
        compiler_params=params,
        cost_estimate=cost,
    )(*args)


def _shift(x, axis, n, d):
    return lax.ppermute(x, axis, [(i, (i + d) % n) for i in range(n)])


def _gather_partition(centroids):
    n_blk = lax.axis_size("blk")
    n_chip = n_blk // 2
    pieces = [centroids]
    for d in range(1, n_chip):
        pairs = [(k * 2 + c, ((k + d) % n_chip) * 2 + c) for k in range(n_chip) for c in range(2)]
        pieces.append(lax.ppermute(centroids, "blk", pairs))
    swap = [(b, b ^ 1) for b in range(n_blk)]
    swapped = [lax.ppermute(p, "blk", swap) for p in pieces]
    return jnp.concatenate(pieces + swapped, axis=0)


def _local(codes, scales, coarse_ids, centroids):
    rows_dev = codes.shape[0]
    width = codes.shape[1]
    loops = lax.axis_size("cell")
    cap = 2 * rows_dev // loops
    me = lax.axis_index("cell")
    dequant = (codes.astype(jnp.float32) * scales[:, None]).astype(jnp.bfloat16)
    onehot = (coarse_ids[:, None] == jnp.arange(loops, dtype=jnp.int32)[None, :]).astype(jnp.int32)
    ranks = jnp.sum(jnp.cumsum(onehot, axis=0) * onehot, axis=1) - 1
    slots = ((coarse_ids - me) % loops) * cap + ranks
    outgoing = jnp.zeros((loops * cap, width), jnp.bfloat16).at[slots].set(dequant)
    outgoing = outgoing.reshape(loops, cap, width)
    part = _gather_partition(centroids)
    arrived = [outgoing[0]] + [_shift(outgoing[d], "cell", loops, d) for d in range(1, loops)]
    real = jnp.sum((coarse_ids == me).astype(jnp.int32))
    remote = jnp.stack(arrived[1:], axis=1).reshape((loops - 1) * cap, width)
    count = ((loops - 1) * real).reshape(1)
    first = soft_part(remote, part, final=True, count=count, tiles=2)
    first = first.reshape(cap, loops - 1, width)
    ret = {d: _shift(first[:, d - 1], "cell", loops, -d) for d in range(1, loops)}
    ret[0] = soft_part(arrived[0], part, final=True)
    back = jnp.concatenate([ret[d] for d in range(loops)], axis=0)
    pick = slots[:, None] == jnp.arange(back.shape[0], dtype=jnp.int32)[None, :]
    mine = jnp.dot(pick.astype(jnp.bfloat16), back, preferred_element_type=jnp.float32)
    mine = mine.astype(jnp.bfloat16)
    residual = (dequant.astype(jnp.float32) - mine.astype(jnp.float32)).astype(jnp.bfloat16)
    return (mine, residual)


def solution(mesh):
    rows = P(("cell", "blk"), None)
    in_specs = (rows, P(("cell", "blk")), P(("cell", "blk")), rows)
    out_specs = (rows, rows)
    return jax.shard_map(_local, mesh=mesh, in_specs=in_specs, out_specs=out_specs, check_vma=False)
```

```python
import functools
import math

import jax
import jax.numpy as jnp
from jax import lax
from jax.experimental import pallas as pl
from jax.experimental.pallas import tpu as pltpu
from jax.sharding import PartitionSpec as P


def _soft_kernel(*refs, chunk, beta, merge, final, counted=False):
    if counted:
        n_ref, refs = refs[0], refs[1:]
        o_ref = refs[2]
        live = pl.program_id(0) * o_ref.shape[0] < n_ref[0]

        @pl.when(live)
        def _():
            _soft_kernel(*refs, chunk=chunk, beta=beta, merge=merge, final=final)

        @pl.when(jnp.logical_not(live))
        def _():
            o_ref[...] = jnp.zeros(o_ref.shape, o_ref.dtype)

        return
    if not merge and final:
        q_ref, c_ref, o_ref, m_sc, l_sc, acc_sc, s_sc = refs
    elif merge:
        q_ref, c_ref, pm_ref, pl_ref, pacc_ref, o_ref, m_sc, l_sc, acc_sc, s_sc = refs
    else:
        q_ref, c_ref, om_ref, ol_ref, oacc_ref, m_sc, l_sc, acc_sc, s_sc = refs
    n_chunks = c_ref.shape[0] // chunk
    lanes = m_sc.shape[1]
    q = q_ref[...]
    m_sc[...] = jnp.full(m_sc.shape, -jnp.inf, jnp.float32)

    @pl.loop(0, n_chunks)
    def _(i):
        cols = pl.ds(pl.multiple_of(i * chunk, chunk), chunk)
        s = lax.dot_general(
            q, c_ref[cols, :], (((1,), (1,)), ((), ())), preferred_element_type=jnp.float32
        ) * beta
        s_sc[:, cols] = s
        m = m_sc[...]
        for j in range(chunk // lanes):
            m = jnp.maximum(m, s[:, j * lanes:(j + 1) * lanes])
        m_sc[...] = m

    top = jnp.max(m_sc[...], axis=1, keepdims=True)
    if merge:
        top = jnp.maximum(top, pm_ref[...])
    l_sc[...] = jnp.zeros(l_sc.shape, jnp.float32)
    acc_sc[...] = jnp.zeros(acc_sc.shape, jnp.float32)

    @pl.loop(0, n_chunks)
    def _(i):
        cols = pl.ds(pl.multiple_of(i * chunk, chunk), chunk)
        w = jnp.exp(s_sc[:, cols] - top).astype(jnp.bfloat16)
        wf = w.astype(jnp.float32)
        l = l_sc[...]
        for j in range(chunk // lanes):
            l = l + wf[:, j * lanes:(j + 1) * lanes]
        l_sc[...] = l
        acc_sc[...] += jnp.dot(w, c_ref[cols, :], preferred_element_type=jnp.float32)

    total = jnp.sum(l_sc[...], axis=1, keepdims=True)
    if final and not merge:
        o_ref[...] = (acc_sc[...] / total).astype(o_ref.dtype)
    elif merge:
        scale = jnp.exp(pm_ref[...] - top)
        total = total + pl_ref[...] * scale
        numer = acc_sc[...] + pacc_ref[...] * scale
        o_ref[...] = (numer / total).astype(o_ref.dtype)
    else:
        om_ref[...] = top
        ol_ref[...] = total
        oacc_ref[...] = acc_sc[...]


def soft_part(queries, cents, prior=None, final=False, count=None, tiles=1):
    slots, width = queries.shape
    n_cent = cents.shape[0]
    chunk = min(4096, n_cent)
    tq = slots // tiles
    while tq * n_cent * 4 > (32 << 20) and tq % 16 == 0:
        tq //= 2
    vmem = 4 * tq * n_cent + 2 * 2 * n_cent * width + 16 * tq * width * 4 + (8 << 20)
    rows = pl.BlockSpec((tq, width), lambda i: (i, 0))
    col = pl.BlockSpec((tq, 1), lambda i: (i, 0))
    in_specs = [rows, pl.BlockSpec((n_cent, width), lambda i: (0, 0))]
    stats = [
        jax.ShapeDtypeStruct((slots, 1), jnp.float32),
        jax.ShapeDtypeStruct((slots, 1), jnp.float32),
        jax.ShapeDtypeStruct((slots, width), jnp.float32),
    ]
    if prior is None and final:
        out_shape = jax.ShapeDtypeStruct((slots, width), jnp.bfloat16)
        out_specs, args = rows, (queries, cents)
    elif prior is None:
        out_shape, out_specs, args = stats, [col, col, rows], (queries, cents)
    else:
        in_specs += [col, col, rows]
        out_shape = jax.ShapeDtypeStruct((slots, width), jnp.bfloat16)
        out_specs, args = rows, (queries, cents) + tuple(prior)
    kernel = functools.partial(
        _soft_kernel,
        chunk=chunk,
        beta=1.0 / math.sqrt(width),
        merge=prior is not None,
        final=final or prior is not None,
        counted=count is not None,
    )
    scratch = [
        pltpu.VMEM((tq, 128), jnp.float32),
        pltpu.VMEM((tq, 128), jnp.float32),
        pltpu.VMEM((tq, width), jnp.float32),
        pltpu.VMEM((tq, n_cent), jnp.float32),
    ]
    params = pltpu.CompilerParams(vmem_limit_bytes=min(vmem, 60 << 20))
    cost = pl.CostEstimate(
        flops=2 * 2 * slots * n_cent * width,
        transcendentals=slots * n_cent,
        bytes_accessed=2 * (2 * slots * width + n_cent * width),
    )
    if count is not None:
        grid_spec = pltpu.PrefetchScalarGridSpec(
            num_scalar_prefetch=1,
            grid=(slots // tq,),
            in_specs=[
                pl.BlockSpec((tq, width), lambda i, n: (i, 0)),
                pl.BlockSpec((n_cent, width), lambda i, n: (0, 0)),
            ],
            out_specs=pl.BlockSpec((tq, width), lambda i, n: (i, 0)),
            scratch_shapes=scratch,
        )
        return pl.pallas_call(
            kernel, out_shape=out_shape, grid_spec=grid_spec, compiler_params=params,
            cost_estimate=cost,
        )(count, *args)
    return pl.pallas_call(
        kernel,
        out_shape=out_shape,
        grid=(slots // tq,),
        in_specs=in_specs,
        out_specs=out_specs,
        scratch_shapes=scratch,
        compiler_params=params,
        cost_estimate=cost,
    )(*args)


def _shift(x, axis, n, d):
    return lax.ppermute(x, axis, [(i, (i + d) % n) for i in range(n)])


def _gather_partition(centroids):
    n_blk = lax.axis_size("blk")
    n_chip = n_blk // 2
    pieces = [centroids]
    for d in range(1, n_chip):
        pairs = [(k * 2 + c, ((k + d) % n_chip) * 2 + c) for k in range(n_chip) for c in range(2)]
        pieces.append(lax.ppermute(centroids, "blk", pairs))
    swap = [(b, b ^ 1) for b in range(n_blk)]
    swapped = [lax.ppermute(p, "blk", swap) for p in pieces]
    return jnp.concatenate(pieces + swapped, axis=0)


def _local(codes, scales, coarse_ids, centroids):
    rows_dev = codes.shape[0]
    width = codes.shape[1]
    loops = lax.axis_size("cell")
    cap = 2 * rows_dev // loops
    me = lax.axis_index("cell")
    dequant = (codes.astype(jnp.float32) * scales[:, None]).astype(jnp.bfloat16)
    onehot = (coarse_ids[:, None] == jnp.arange(loops, dtype=jnp.int32)[None, :]).astype(jnp.int32)
    ranks = jnp.sum(jnp.cumsum(onehot, axis=0) * onehot, axis=1) - 1
    slots = ((coarse_ids - me) % loops) * cap + ranks
    outgoing = jnp.zeros((loops * cap, width), jnp.bfloat16).at[slots].set(dequant)
    outgoing = outgoing.reshape(loops, cap, width)
    part = _gather_partition(centroids)
    arrived = [outgoing[0]] + [_shift(outgoing[d], "cell", loops, d) for d in range(1, loops)]
    real = jnp.sum((coarse_ids == me).astype(jnp.int32))
    remote = jnp.stack(arrived[1:], axis=1).reshape((loops - 1) * cap, width)
    count = ((loops - 1) * real).reshape(1)
    half = remote.shape[0] // 2
    first = lax.cond(
        count[0] > half,
        lambda q, c, n: soft_part(q, c, final=True),
        lambda q, c, n: soft_part(q, c, final=True, count=n, tiles=2),
        remote,
        part,
        count,
    )
    first = first.reshape(cap, loops - 1, width)
    ret = {d: _shift(first[:, d - 1], "cell", loops, -d) for d in range(1, loops)}
    ret[0] = soft_part(arrived[0], part, final=True)
    back = jnp.concatenate([ret[d] for d in range(loops)], axis=0)
    pick = slots[:, None] == jnp.arange(back.shape[0], dtype=jnp.int32)[None, :]
    mine = jnp.dot(pick.astype(jnp.bfloat16), back, preferred_element_type=jnp.float32)
    mine = mine.astype(jnp.bfloat16)
    residual = (dequant.astype(jnp.float32) - mine.astype(jnp.float32)).astype(jnp.bfloat16)
    return (mine, residual)


def solution(mesh):
    rows = P(("cell", "blk"), None)
    in_specs = (rows, P(("cell", "blk")), P(("cell", "blk")), rows)
    out_specs = (rows, rows)
    return jax.shard_map(_local, mesh=mesh, in_specs=in_specs, out_specs=out_specs, check_vma=False)
```

```python
import functools
import math

import jax
import jax.numpy as jnp
from jax import lax
from jax.experimental import pallas as pl
from jax.experimental.pallas import tpu as pltpu
from jax.sharding import PartitionSpec as P


def _soft_kernel(*refs, chunk, beta, merge, final):
    if not merge and final:
        q_ref, c_ref, o_ref, m_sc, l_sc, acc_sc, s_sc = refs
    elif merge:
        q_ref, c_ref, pm_ref, pl_ref, pacc_ref, o_ref, m_sc, l_sc, acc_sc, s_sc = refs
    else:
        q_ref, c_ref, om_ref, ol_ref, oacc_ref, m_sc, l_sc, acc_sc, s_sc = refs
    n_chunks = c_ref.shape[0] // chunk
    lanes = m_sc.shape[1]
    q = q_ref[...]
    m_sc[...] = jnp.full(m_sc.shape, -jnp.inf, jnp.float32)

    @pl.loop(0, n_chunks)
    def _(i):
        cols = pl.ds(pl.multiple_of(i * chunk, chunk), chunk)
        s = lax.dot_general(
            q, c_ref[cols, :], (((1,), (1,)), ((), ())), preferred_element_type=jnp.float32
        ) * beta
        s_sc[:, cols] = s
        m = m_sc[...]
        for j in range(chunk // lanes):
            m = jnp.maximum(m, s[:, j * lanes:(j + 1) * lanes])
        m_sc[...] = m

    top = jnp.max(m_sc[...], axis=1, keepdims=True)
    if merge:
        top = jnp.maximum(top, pm_ref[...])
    l_sc[...] = jnp.zeros(l_sc.shape, jnp.float32)
    acc_sc[...] = jnp.zeros(acc_sc.shape, jnp.float32)

    @pl.loop(0, n_chunks)
    def _(i):
        cols = pl.ds(pl.multiple_of(i * chunk, chunk), chunk)
        w = jnp.exp(s_sc[:, cols] - top).astype(jnp.bfloat16)
        wf = w.astype(jnp.float32)
        l = l_sc[...]
        for j in range(chunk // lanes):
            l = l + wf[:, j * lanes:(j + 1) * lanes]
        l_sc[...] = l
        acc_sc[...] += jnp.dot(w, c_ref[cols, :], preferred_element_type=jnp.float32)

    total = jnp.sum(l_sc[...], axis=1, keepdims=True)
    if final and not merge:
        o_ref[...] = (acc_sc[...] / total).astype(o_ref.dtype)
    elif merge:
        scale = jnp.exp(pm_ref[...] - top)
        total = total + pl_ref[...] * scale
        numer = acc_sc[...] + pacc_ref[...] * scale
        o_ref[...] = (numer / total).astype(o_ref.dtype)
    else:
        om_ref[...] = top
        ol_ref[...] = total
        oacc_ref[...] = acc_sc[...]


def soft_part(queries, cents, prior=None, final=False):
    slots, width = queries.shape
    n_cent = cents.shape[0]
    chunk = min(4096, n_cent)
    tq = slots
    while tq * n_cent * 4 > (32 << 20) and tq % 16 == 0:
        tq //= 2
    vmem = 4 * tq * n_cent + 2 * 2 * n_cent * width + 16 * tq * width * 4 + (8 << 20)
    rows = pl.BlockSpec((tq, width), lambda i: (i, 0))
    col = pl.BlockSpec((tq, 1), lambda i: (i, 0))
    in_specs = [rows, pl.BlockSpec((n_cent, width), lambda i: (0, 0))]
    stats = [
        jax.ShapeDtypeStruct((slots, 1), jnp.float32),
        jax.ShapeDtypeStruct((slots, 1), jnp.float32),
        jax.ShapeDtypeStruct((slots, width), jnp.float32),
    ]
    if prior is None and final:
        out_shape = jax.ShapeDtypeStruct((slots, width), jnp.bfloat16)
        out_specs, args = rows, (queries, cents)
    elif prior is None:
        out_shape, out_specs, args = stats, [col, col, rows], (queries, cents)
    else:
        in_specs += [col, col, rows]
        out_shape = jax.ShapeDtypeStruct((slots, width), jnp.bfloat16)
        out_specs, args = rows, (queries, cents) + tuple(prior)
    return pl.pallas_call(
        functools.partial(
            _soft_kernel,
            chunk=chunk,
            beta=1.0 / math.sqrt(width),
            merge=prior is not None,
            final=final or prior is not None,
        ),
        out_shape=out_shape,
        grid=(slots // tq,),
        in_specs=in_specs,
        out_specs=out_specs,
        scratch_shapes=[
            pltpu.VMEM((tq, 128), jnp.float32),
            pltpu.VMEM((tq, 128), jnp.float32),
            pltpu.VMEM((tq, width), jnp.float32),
            pltpu.VMEM((tq, n_cent), jnp.float32),
        ],
        compiler_params=pltpu.CompilerParams(vmem_limit_bytes=min(vmem, 60 << 20)),
        cost_estimate=pl.CostEstimate(
            flops=2 * 2 * slots * n_cent * width,
            transcendentals=slots * n_cent,
            bytes_accessed=2 * (2 * slots * width + n_cent * width),
        ),
    )(*args)


def _shift(x, axis, n, d):
    return lax.ppermute(x, axis, [(i, (i + d) % n) for i in range(n)])


def _gather_partition(centroids):
    n_blk = lax.axis_size("blk")
    n_chip = n_blk // 2
    pieces = [centroids]
    for d in sorted(range(1, n_chip), key=lambda d: -min(d, n_chip - d) * 10 - d):
        pairs = [(k * 2 + c, ((k + d) % n_chip) * 2 + c) for k in range(n_chip) for c in range(2)]
        pieces.append(lax.ppermute(centroids, "blk", pairs))
    swap = [(b, b ^ 1) for b in range(n_blk)]
    swapped = [lax.ppermute(p, "blk", swap) for p in pieces]
    return jnp.concatenate(pieces + swapped, axis=0)


def _local(codes, scales, coarse_ids, centroids):
    rows_dev = codes.shape[0]
    width = codes.shape[1]
    loops = lax.axis_size("cell")
    cap = 2 * rows_dev // loops
    me = lax.axis_index("cell")
    dequant = (codes.astype(jnp.float32) * scales[:, None]).astype(jnp.bfloat16)
    onehot = (coarse_ids[:, None] == jnp.arange(loops, dtype=jnp.int32)[None, :]).astype(jnp.int32)
    ranks = jnp.sum(jnp.cumsum(onehot, axis=0) * onehot, axis=1) - 1
    slots = ((coarse_ids - me) % loops) * cap + ranks
    outgoing = jnp.zeros((loops * cap, width), jnp.bfloat16).at[slots].set(dequant)
    outgoing = outgoing.reshape(loops, cap, width)
    part = _gather_partition(centroids)
    arrived = [outgoing[0]] + [_shift(outgoing[d], "cell", loops, d) for d in range(1, loops)]
    first = soft_part(jnp.concatenate(arrived[1:], axis=0), part, final=True)
    ret = {d: _shift(first[(d - 1) * cap:d * cap], "cell", loops, -d) for d in range(1, loops)}
    ret[0] = soft_part(arrived[0], part, final=True)
    back = jnp.concatenate([ret[d] for d in range(loops)], axis=0)
    pick = slots[:, None] == jnp.arange(back.shape[0], dtype=jnp.int32)[None, :]
    mine = jnp.dot(pick.astype(jnp.bfloat16), back, preferred_element_type=jnp.float32)
    mine = mine.astype(jnp.bfloat16)
    residual = (dequant.astype(jnp.float32) - mine.astype(jnp.float32)).astype(jnp.bfloat16)
    return (mine, residual)


def solution(mesh):
    rows = P(("cell", "blk"), None)
    in_specs = (rows, P(("cell", "blk")), P(("cell", "blk")), rows)
    out_specs = (rows, rows)
    return jax.shard_map(_local, mesh=mesh, in_specs=in_specs, out_specs=out_specs, check_vma=False)
```

```python
import functools
import math

import jax
import jax.numpy as jnp
from jax import lax
from jax.experimental import pallas as pl
from jax.experimental.pallas import tpu as pltpu
from jax.sharding import PartitionSpec as P


def _soft_kernel(*refs, chunk, beta, merge, final):
    if not merge and final:
        q_ref, c_ref, o_ref, m_sc, l_sc, acc_sc, s_sc = refs
    elif merge:
        q_ref, c_ref, pm_ref, pl_ref, pacc_ref, o_ref, m_sc, l_sc, acc_sc, s_sc = refs
    else:
        q_ref, c_ref, om_ref, ol_ref, oacc_ref, m_sc, l_sc, acc_sc, s_sc = refs
    n_chunks = c_ref.shape[0] // chunk
    lanes = m_sc.shape[1]
    q = q_ref[...]
    m_sc[...] = jnp.full(m_sc.shape, -jnp.inf, jnp.float32)

    @pl.loop(0, n_chunks)
    def _(i):
        cols = pl.ds(pl.multiple_of(i * chunk, chunk), chunk)
        s = lax.dot_general(
            q, c_ref[cols, :], (((1,), (1,)), ((), ())), preferred_element_type=jnp.float32
        ) * beta
        s_sc[:, cols] = s
        m = m_sc[...]
        for j in range(chunk // lanes):
            m = jnp.maximum(m, s[:, j * lanes:(j + 1) * lanes])
        m_sc[...] = m

    top = jnp.max(m_sc[...], axis=1, keepdims=True)
    if merge:
        top = jnp.maximum(top, pm_ref[...])
    l_sc[...] = jnp.zeros(l_sc.shape, jnp.float32)
    acc_sc[...] = jnp.zeros(acc_sc.shape, jnp.float32)

    @pl.loop(0, n_chunks)
    def _(i):
        cols = pl.ds(pl.multiple_of(i * chunk, chunk), chunk)
        w = jnp.exp(s_sc[:, cols] - top).astype(jnp.bfloat16)
        wf = w.astype(jnp.float32)
        l = l_sc[...]
        for j in range(chunk // lanes):
            l = l + wf[:, j * lanes:(j + 1) * lanes]
        l_sc[...] = l
        acc_sc[...] += jnp.dot(w, c_ref[cols, :], preferred_element_type=jnp.float32)

    total = jnp.sum(l_sc[...], axis=1, keepdims=True)
    if final and not merge:
        o_ref[...] = (acc_sc[...] / total).astype(o_ref.dtype)
    elif merge:
        scale = jnp.exp(pm_ref[...] - top)
        total = total + pl_ref[...] * scale
        numer = acc_sc[...] + pacc_ref[...] * scale
        o_ref[...] = (numer / total).astype(o_ref.dtype)
    else:
        om_ref[...] = top
        ol_ref[...] = total
        oacc_ref[...] = acc_sc[...]


def soft_part(queries, cents, prior=None, final=False):
    slots, width = queries.shape
    n_cent = cents.shape[0]
    chunk = min(4096, n_cent)
    tq = slots
    while tq * n_cent * 4 > (32 << 20) and tq % 16 == 0:
        tq //= 2
    vmem = 4 * tq * n_cent + 2 * 2 * n_cent * width + 16 * tq * width * 4 + (8 << 20)
    rows = pl.BlockSpec((tq, width), lambda i: (i, 0))
    col = pl.BlockSpec((tq, 1), lambda i: (i, 0))
    in_specs = [rows, pl.BlockSpec((n_cent, width), lambda i: (0, 0))]
    stats = [
        jax.ShapeDtypeStruct((slots, 1), jnp.float32),
        jax.ShapeDtypeStruct((slots, 1), jnp.float32),
        jax.ShapeDtypeStruct((slots, width), jnp.float32),
    ]
    if prior is None and final:
        out_shape = jax.ShapeDtypeStruct((slots, width), jnp.bfloat16)
        out_specs, args = rows, (queries, cents)
    elif prior is None:
        out_shape, out_specs, args = stats, [col, col, rows], (queries, cents)
    else:
        in_specs += [col, col, rows]
        out_shape = jax.ShapeDtypeStruct((slots, width), jnp.bfloat16)
        out_specs, args = rows, (queries, cents) + tuple(prior)
    return pl.pallas_call(
        functools.partial(
            _soft_kernel,
            chunk=chunk,
            beta=1.0 / math.sqrt(width),
            merge=prior is not None,
            final=final or prior is not None,
        ),
        out_shape=out_shape,
        grid=(slots // tq,),
        in_specs=in_specs,
        out_specs=out_specs,
        scratch_shapes=[
            pltpu.VMEM((tq, 128), jnp.float32),
            pltpu.VMEM((tq, 128), jnp.float32),
            pltpu.VMEM((tq, width), jnp.float32),
            pltpu.VMEM((tq, n_cent), jnp.float32),
        ],
        compiler_params=pltpu.CompilerParams(vmem_limit_bytes=min(vmem, 60 << 20)),
        cost_estimate=pl.CostEstimate(
            flops=2 * 2 * slots * n_cent * width,
            transcendentals=slots * n_cent,
            bytes_accessed=2 * (2 * slots * width + n_cent * width),
        ),
    )(*args)


def _shift(x, axis, n, d):
    return lax.ppermute(x, axis, [(i, (i + d) % n) for i in range(n)])


def _gather_partition(centroids):
    n_blk = lax.axis_size("blk")
    n_chip = n_blk // 2
    pieces = [centroids]
    for d in sorted(range(1, n_chip), key=lambda d: -min(d, n_chip - d) * 10 - d):
        pairs = [(k * 2 + c, ((k + d) % n_chip) * 2 + c) for k in range(n_chip) for c in range(2)]
        pieces.append(lax.ppermute(centroids, "blk", pairs))
    swap = [(b, b ^ 1) for b in range(n_blk)]
    swapped = [lax.ppermute(p, "blk", swap) for p in pieces]
    return jnp.concatenate(pieces + swapped, axis=0)


def _local(codes, scales, coarse_ids, centroids):
    rows_dev = codes.shape[0]
    width = codes.shape[1]
    loops = lax.axis_size("cell")
    cap = 2 * rows_dev // loops
    me = lax.axis_index("cell")
    dequant = (codes.astype(jnp.float32) * scales[:, None]).astype(jnp.bfloat16)
    onehot = (coarse_ids[:, None] == jnp.arange(loops, dtype=jnp.int32)[None, :]).astype(jnp.int32)
    ranks = jnp.sum(jnp.cumsum(onehot, axis=0) * onehot, axis=1) - 1
    slots = ((coarse_ids - me) % loops) * cap + ranks
    outgoing = jnp.zeros((loops * cap, width), jnp.bfloat16).at[slots].set(dequant)
    outgoing = outgoing.reshape(loops, cap, width)
    part = _gather_partition(centroids)
    arrived = [outgoing[0]] + [_shift(outgoing[d], "cell", loops, d) for d in range(1, loops)]
    first = soft_part(jnp.concatenate(arrived[1:], axis=0), part, final=True)
    ret = {d: _shift(first[(d - 1) * cap:d * cap], "cell", loops, -d) for d in range(1, loops)}
    ret[0] = soft_part(arrived[0], part, final=True)
    pick = (slots[:, None] == jnp.arange(loops * cap, dtype=jnp.int32)[None, :]).astype(jnp.bfloat16)
    own = jnp.dot(pick[:, :cap], ret[0], preferred_element_type=jnp.float32)
    remote = jnp.concatenate([ret[d] for d in range(1, loops)], axis=0)
    mine = own + jnp.dot(pick[:, cap:], remote, preferred_element_type=jnp.float32)
    mine = mine.astype(jnp.bfloat16)
    residual = (dequant.astype(jnp.float32) - mine.astype(jnp.float32)).astype(jnp.bfloat16)
    return (mine, residual)


def solution(mesh):
    rows = P(("cell", "blk"), None)
    in_specs = (rows, P(("cell", "blk")), P(("cell", "blk")), rows)
    out_specs = (rows, rows)
    return jax.shard_map(_local, mesh=mesh, in_specs=in_specs, out_specs=out_specs, check_vma=False)
```
